256 devices in a mesh: ctx: 32 (over z, y_hi, core), mp: 8 (over x, y_lo).
Axes of the slice: x: 4, y: 4 (y_hi: 2, y_lo: 2; y = y_hi * 2 + y_lo), z: 8, core: 2. Of those that a mesh axis runs over, the one named last changes fastest.
Arguments:
- proj: bfloat16 [8192, 3, 8192], P(('ctx', 'mp')), may hold values from -6 to 6
- conv_weight: float32 [3, 7, 8192], replicated, may hold values from -2 to 2
- residues: float32 [128, 16], P('mp'), may hold values from -1.5 to 1.5
- decays: float32 [128, 16], P('mp'), may hold values from 1.2207031e-05 to 0.03
- doc_lengths: int32 [64], replicated, may hold values from 1 to 768, 8192 in all
Outputs:
- mixed: bfloat16 [8192, 8192], P(('ctx', 'mp'))
The draws below stay inside these ranges and needn't reach their ends.
All inputs are finite; a program needn't handle non-finite values.
Results may differ from the reference program's by a relative error of at most 0.014.
Values may be sent and summed in bfloat16 or wider, within the bound.
No kernel may reach another device: no remote copies, remote signals or barrier semaphores. Data moves between devices by JAX's collectives and lax.ppermute only.
A program may use at most 64 MiB of HBM per device.

```python
import math
import jax
import jax.numpy as jnp
import numpy as np
from jax import lax

D = 8192
GSIZE = 64
MODES = 16
KERNEL = 7
TOK_DEV = 256
GROUPS = 128
TOKENS = 8192
DOCS = 64


def level_of(rng, shape, cuts, least, high):
    def one(position, parts):
        heights = jax.random.uniform(jax.random.fold_in(jax.random.fold_in(rng, 6), position), (parts,), jnp.float32, least / len(cuts), high / len(cuts))
        return jnp.repeat(jnp.exp(heights), shape[position] // parts).reshape((-1,) + (1,) * (len(shape) - position - 1))

    loudness = one(*cuts[0])
    for cut in cuts[1:]:
        loudness = loudness * one(*cut)
    return loudness


def length_profile(amount, total, bound, slope):
    weights = [(1 << 20) // math.isqrt(rank ** slope) + 1 for rank in range(2, amount + 1)]
    spare, counts = total - bound - (amount - 1), [1] * (amount - 1)
    while spare > 0:
        candidates = [i for i in range(amount - 1) if counts[i] < bound]
        pool, remaining = sum([weights[i] for i in candidates]), spare
        for i in candidates:
            extra = min(bound - counts[i], max(1, remaining * weights[i] // pool), spare)
            counts[i] = counts[i] + extra
            spare = spare - extra
    return np.array([bound] + counts)


def ragged_sizes(key, number_of, total, most, skew):
    if number_of == 2:
        one = jax.random.randint(key, (), max(1, total - most), min(most, total - 1) + 1)
        return jnp.stack([one, total - one])
    sizes = jnp.asarray(length_profile(number_of, total, most, skew), jnp.int32)
    couples = (number_of - 1) // 2
    donor, receiver = sizes[1:1 + 2 * couples:2], sizes[2:2 + 2 * couples:2]
    room = jnp.minimum(donor - 1, most - receiver)
    shifted = jax.random.randint(jax.random.fold_in(key, 1), (couples,), 0, 1 << 20) % (room + 1)
    sizes = sizes.at[1:1 + 2 * couples:2].set(donor - shifted).at[2:2 + 2 * couples:2].set(receiver + shifted)
    return sizes[jax.random.permutation(jax.random.fold_in(key, 2), number_of)]


def normal_values(own_key, shape, deviation, bound, shards=(), held_as=jnp.bfloat16):
    values = deviation * jax.random.normal(own_key, shape, jnp.float32)
    if shards:
        values = values * level_of(own_key, shape, shards, -0.22, 0.18)
    return jnp.clip(values, -bound, bound).astype(held_as)


def setup_inputs(seed: int = 0) -> dict:
    splits = jax.random.split(jax.random.key(seed), 6)
    proj = normal_values(splits[0], (TOKENS, 3, D), 1.0, 6.0, ((0, 256),))
    conv_weight = normal_values(splits[1], (3, KERNEL, D), 0.4, 2.0, (), jnp.float32)
    residues = normal_values(splits[2], (GROUPS, MODES), 0.25, 1.5, ((0, 8),), jnp.float32)
    decays = jnp.clip(jnp.exp(math.log(0.03) - 7.8069405 * jax.random.uniform(splits[3], (GROUPS, MODES), jnp.float32) ** level_of(splits[3], (GROUPS, MODES), ((0, 8),), -0.2, 0.2)), 1.220703143189894e-05, 0.03)
    doc_lengths = ragged_sizes(splits[4], DOCS, TOKENS, 3 * TOK_DEV, 1).astype(jnp.int32)
    return dict(proj=proj, conv_weight=conv_weight, residues=residues, decays=decays, doc_lengths=doc_lengths)


def document_number_index(doc_lengths, positions):
    doc_starts = jnp.cumsum(doc_lengths) - doc_lengths
    inside = (doc_starts[None, :] <= positions[:, None]).astype(jnp.int32)
    return (lax.optimization_barrier(jnp.sum(inside, axis=1)) - 1).astype(jnp.int32)

def short_convolution(padded, conv_weight, padded_document_ids, padded_pos, out_rows):
    kernel_len = conv_weight.shape[1]
    result = jnp.zeros((out_rows,) + padded.shape[1:], jnp.float32)
    own_docs = padded_document_ids[kernel_len - 1:]
    for position_shift in range(kernel_len):
        begin_row = kernel_len - 1 - position_shift
        earlier = padded[begin_row:begin_row + out_rows].astype(jnp.float32)
        keep_mask = (padded_document_ids[begin_row:begin_row + out_rows] == own_docs) & (padded_pos[begin_row:begin_row + out_rows] >= 0)
        result = result + conv_weight[:, position_shift, :][None] * earlier * keep_mask.astype(jnp.float32)[:, None, None]
    return result

def filter_taps(residues, decays, lag_values):
    coefficient = residues * jnp.sqrt(decays)
    powers = jnp.exp(-decays[:, :, None] * lag_values[None, None, :])
    return jnp.einsum('gm,gmt->gt', coefficient, powers, precision=lax.Precision.HIGHEST)

def reference(proj, conv_weight, residues, decays, doc_lengths):
    padded_pos = (jnp.arange(TOKENS + KERNEL - 1) - (KERNEL - 1)).astype(jnp.int32)
    padded_document_ids = document_number_index(doc_lengths, padded_pos)
    padded = jnp.pad(proj, ((KERNEL - 1, 0), (0, 0), (0, 0)))
    conv = short_convolution(padded, conv_weight, padded_document_ids, padded_pos, TOKENS)
    query_part = conv[:, 0]
    product = (conv[:, 1] * conv[:, 2]).astype(jnp.bfloat16)
    lag_values = jnp.arange(TOKENS).astype(jnp.float32)
    tap_table = filter_taps(residues, decays, lag_values)
    grouped = product.astype(jnp.float32).reshape(TOKENS, GROUPS, GSIZE).transpose(1, 0, 2)

    def one_group(group_pair):
        tap_row, inputs = group_pair
        length = 2 * TOKENS
        spectrum = jnp.fft.rfft(tap_row, length)[:, None] * jnp.fft.rfft(inputs, length, axis=0)
        return jnp.fft.irfft(spectrum, length, axis=0)[:TOKENS].astype(jnp.float32)
    filtered = lax.map(one_group, (tap_table, grouped))
    filtered = filtered.transpose(1, 0, 2).reshape(TOKENS, D).astype(jnp.bfloat16)
    return (query_part * filtered.astype(jnp.float32)).astype(jnp.bfloat16)
```

```python
import jax
import jax.numpy as jnp
from jax import lax
from jax.sharding import PartitionSpec as P

HIGHEST = lax.Precision.HIGHEST


def shifted(block, axis, distance):
    count = lax.axis_size(axis)
    route = [(i, i + distance) for i in range(count - distance)]
    return lax.ppermute(block, axis, route)


def document_number_index(doc_lengths, positions):
    doc_starts = jnp.cumsum(doc_lengths) - doc_lengths
    inside = (doc_starts[None, :] <= positions[:, None]).astype(jnp.int32)
    return jnp.sum(inside, axis=1) - 1


def short_convolution(padded, conv_weight, padded_document_ids, padded_pos, out_rows):
    kernel_len = conv_weight.shape[1]
    result = jnp.zeros((out_rows,) + padded.shape[1:], jnp.float32)
    own_docs = padded_document_ids[kernel_len - 1 :]
    for position_shift in range(kernel_len):
        begin_row = kernel_len - 1 - position_shift
        earlier = padded[begin_row : begin_row + out_rows].astype(jnp.float32)
        keep_mask = (padded_document_ids[begin_row : begin_row + out_rows] == own_docs) & (
            padded_pos[begin_row : begin_row + out_rows] >= 0
        )
        result = (
            result
            + conv_weight[:, position_shift, :][None]
            * earlier
            * keep_mask.astype(jnp.float32)[:, None, None]
        )
    return result


def split_product(form, weights, inputs):
    upper_part = weights.astype(jnp.bfloat16)
    lower_part = (weights - upper_part.astype(jnp.float32)).astype(jnp.bfloat16)
    first = jnp.einsum(form, upper_part, inputs, preferred_element_type=jnp.float32)
    return first + jnp.einsum(form, lower_part, inputs, preferred_element_type=jnp.float32)


def long_filter(product, residues, decays):
    block_len, channels = product.shape
    group_count = residues.shape[0]
    group_width = channels // group_count
    coefficient = residues * jnp.sqrt(decays)
    offsets = jnp.arange(block_len, dtype=jnp.float32)
    left = coefficient[:, None, :] * jnp.exp(-decays[:, None, :] * offsets[None, :, None])
    right = jnp.exp(decays[:, :, None] * offsets[None, None, :])
    tile = jnp.einsum("grm,gms->grs", left, right, precision=HIGHEST)
    lag = jnp.arange(block_len)[:, None] - jnp.arange(block_len)[None, :]
    tile = jnp.where((lag >= 0)[None], tile, 0.0)
    inputs = product.reshape(block_len, group_count, group_width)
    intra = split_product("grs,sgc->rgc", tile, inputs)

    end_weight = jnp.exp(-decays[:, :, None] * (float(block_len) - offsets)[None, None, :])
    local_state = split_product("gms,sgc->gmc", end_weight, inputs)

    state = shifted(local_state, "ctx", 1)
    count = lax.axis_size("ctx")
    distance = 1
    while distance < count:
        decay_k = jnp.exp(-decays * float(block_len * distance))
        state = state + decay_k[:, :, None] * shifted(state, "ctx", distance)
        distance *= 2

    inter = jnp.einsum("grm,gmc->rgc", left, state, precision=HIGHEST)
    return (intra + inter).reshape(block_len, channels).astype(jnp.bfloat16)


def shards(proj, conv_weight, residues, decays, doc_lengths):
    kernel_len = conv_weight.shape[1]
    rows = proj.shape[0]
    lin_axis = ("ctx", "mp")
    tail_rows = shifted(proj[rows - (kernel_len - 1) :], lin_axis, 1)
    lin_index = lax.axis_index("ctx") * lax.axis_size("mp") + lax.axis_index("mp")
    padded_pos = lin_index * rows - (kernel_len - 1) + jnp.arange(rows + kernel_len - 1, dtype=jnp.int32)
    padded_document_ids = document_number_index(doc_lengths, padded_pos)
    padded = jnp.concatenate([tail_rows, proj], axis=0)
    conv = short_convolution(padded, conv_weight, padded_document_ids, padded_pos, rows)
    query_part = conv[:, 0]
    product = (conv[:, 1] * conv[:, 2]).astype(jnp.bfloat16)
    channel_rows = lax.all_to_all(product, "mp", split_axis=1, concat_axis=0, tiled=True)
    filtered = long_filter(channel_rows, residues, decays)
    filtered = lax.all_to_all(filtered, "mp", split_axis=0, concat_axis=1, tiled=True)
    return (query_part * filtered.astype(jnp.float32)).astype(jnp.bfloat16)


def solution(mesh):
    return jax.shard_map(
        shards,
        mesh=mesh,
        in_specs=(P(("ctx", "mp"), None, None), P(), P("mp", None), P("mp", None), P()),
        out_specs=P(("ctx", "mp"), None),
        check_vma=False,
    )
```

```python
import jax
import jax.numpy as jnp
from jax import lax
from jax.sharding import PartitionSpec as P

HIGHEST = lax.Precision.HIGHEST


def shifted(block, axis, distance):
    count = lax.axis_size(axis)
    route = [(i, i + distance) for i in range(count - distance)]
    return lax.ppermute(block, axis, route)


def document_number_index(doc_lengths, positions):
    doc_starts = jnp.cumsum(doc_lengths) - doc_lengths
    inside = (doc_starts[None, :] <= positions[:, None]).astype(jnp.int32)
    return jnp.sum(inside, axis=1) - 1


def short_convolution(padded, conv_weight, padded_document_ids, padded_pos, out_rows):
    kernel_len = conv_weight.shape[1]
    result = jnp.zeros((out_rows,) + padded.shape[1:], jnp.float32)
    own_docs = padded_document_ids[kernel_len - 1 :]
    for position_shift in range(kernel_len):
        begin_row = kernel_len - 1 - position_shift
        earlier = padded[begin_row : begin_row + out_rows].astype(jnp.float32)
        keep_mask = (padded_document_ids[begin_row : begin_row + out_rows] == own_docs) & (
            padded_pos[begin_row : begin_row + out_rows] >= 0
        )
        result = (
            result
            + conv_weight[:, position_shift, :][None]
            * earlier
            * keep_mask.astype(jnp.float32)[:, None, None]
        )
    return result


def split_product(form, weights, inputs):
    upper_part = weights.astype(jnp.bfloat16)
    lower_part = (weights - upper_part.astype(jnp.float32)).astype(jnp.bfloat16)
    first = jnp.einsum(form, upper_part, inputs, preferred_element_type=jnp.float32)
    return first + jnp.einsum(form, lower_part, inputs, preferred_element_type=jnp.float32)


def long_filter(product, residues, decays):
    block_len, channels = product.shape
    group_count = residues.shape[0]
    group_width = channels // group_count
    coefficient = residues * jnp.sqrt(decays)
    offsets = jnp.arange(block_len, dtype=jnp.float32)
    left = coefficient[:, None, :] * jnp.exp(-decays[:, None, :] * offsets[None, :, None])
    right = jnp.exp(decays[:, :, None] * offsets[None, None, :])
    tile = jnp.einsum("grm,gms->grs", left, right, precision=HIGHEST)
    lag = jnp.arange(block_len)[:, None] - jnp.arange(block_len)[None, :]
    tile = jnp.where((lag >= 0)[None], tile, 0.0)
    inputs = product.reshape(block_len, group_count, group_width)
    intra = split_product("grs,sgc->rgc", tile, inputs)

    end_weight = jnp.exp(-decays[:, :, None] * (float(block_len) - offsets)[None, None, :])
    local_state = split_product("gms,sgc->gmc", end_weight, inputs)

    gathered = lax.all_gather(local_state, "ctx", axis=0)
    count = gathered.shape[0]
    here = lax.axis_index("ctx")
    earlier = jnp.arange(count, dtype=jnp.int32)
    gap = (here - 1 - earlier).astype(jnp.float32) * float(block_len)
    weight = jnp.where(
        (earlier < here)[:, None, None],
        jnp.exp(-decays[None] * jnp.maximum(gap, 0.0)[:, None, None]),
        0.0,
    )
    state = jnp.sum(weight[:, :, :, None] * gathered, axis=0)

    inter = jnp.einsum("grm,gmc->rgc", left, state, precision=HIGHEST)
    return (intra + inter).reshape(block_len, channels).astype(jnp.bfloat16)


def shards(proj, conv_weight, residues, decays, doc_lengths):
    kernel_len = conv_weight.shape[1]
    rows = proj.shape[0]
    lin_axis = ("ctx", "mp")
    tail_rows = shifted(proj[rows - (kernel_len - 1) :], lin_axis, 1)
    lin_index = lax.axis_index("ctx") * lax.axis_size("mp") + lax.axis_index("mp")
    padded_pos = lin_index * rows - (kernel_len - 1) + jnp.arange(rows + kernel_len - 1, dtype=jnp.int32)
    padded_document_ids = document_number_index(doc_lengths, padded_pos)
    padded = jnp.concatenate([tail_rows, proj], axis=0)
    conv = short_convolution(padded, conv_weight, padded_document_ids, padded_pos, rows)
    query_part = conv[:, 0]
    product = (conv[:, 1] * conv[:, 2]).astype(jnp.bfloat16)
    channel_rows = lax.all_to_all(product, "mp", split_axis=1, concat_axis=0, tiled=True)
    filtered = long_filter(channel_rows, residues, decays)
    filtered = lax.all_to_all(filtered, "mp", split_axis=0, concat_axis=1, tiled=True)
    return (query_part * filtered.astype(jnp.float32)).astype(jnp.bfloat16)


def solution(mesh):
    return jax.shard_map(
        shards,
        mesh=mesh,
        in_specs=(P(("ctx", "mp"), None, None), P(), P("mp", None), P("mp", None), P()),
        out_specs=P(("ctx", "mp"), None),
        check_vma=False,
    )
```

```python
import jax
import jax.numpy as jnp
from jax import lax
from jax.sharding import PartitionSpec as P

HIGHEST = lax.Precision.HIGHEST


def shifted(block, axis, distance):
    count = lax.axis_size(axis)
    route = [(i, i + distance) for i in range(count - distance)]
    return lax.ppermute(block, axis, route)


def document_number_index(doc_lengths, positions):
    doc_starts = jnp.cumsum(doc_lengths) - doc_lengths
    inside = (doc_starts[None, :] <= positions[:, None]).astype(jnp.int32)
    return jnp.sum(inside, axis=1) - 1


def short_convolution(padded, conv_weight, padded_document_ids, padded_pos, out_rows):
    kernel_len = conv_weight.shape[1]
    result = jnp.zeros((out_rows,) + padded.shape[1:], jnp.float32)
    own_docs = padded_document_ids[kernel_len - 1 :]
    for position_shift in range(kernel_len):
        begin_row = kernel_len - 1 - position_shift
        earlier = padded[begin_row : begin_row + out_rows].astype(jnp.float32)
        keep_mask = (padded_document_ids[begin_row : begin_row + out_rows] == own_docs) & (
            padded_pos[begin_row : begin_row + out_rows] >= 0
        )
        result = (
            result
            + conv_weight[:, position_shift, :][None]
            * earlier
            * keep_mask.astype(jnp.float32)[:, None, None]
        )
    return result


def split_product(form, weights, inputs):
    upper_part = weights.astype(jnp.bfloat16)
    lower_part = (weights - upper_part.astype(jnp.float32)).astype(jnp.bfloat16)
    first = jnp.einsum(form, upper_part, inputs, preferred_element_type=jnp.float32)
    return first + jnp.einsum(form, lower_part, inputs, preferred_element_type=jnp.float32)


def long_filter(product, coefficient, decays, block_len):
    positions, channels = product.shape
    block_count = positions // block_len
    offsets = jnp.arange(block_len, dtype=jnp.float32)
    left = coefficient[None, :] * jnp.exp(-decays[None, :] * offsets[:, None])
    right = jnp.exp(decays[:, None] * offsets[None, :])
    tile = jnp.dot(left, right, precision=HIGHEST)
    lag = jnp.arange(block_len)[:, None] - jnp.arange(block_len)[None, :]
    tile = jnp.where(lag >= 0, tile, 0.0)
    inputs = product.reshape(block_count, block_len, channels)
    intra = split_product("rs,bsc->brc", tile, inputs)

    end_weight = jnp.exp(-decays[:, None] * (float(block_len) - offsets)[None, :])
    local_state = split_product("ms,bsc->mbc", end_weight, inputs)

    later = jnp.arange(block_count)[:, None]
    earlier = jnp.arange(block_count)[None, :]
    gap = jnp.maximum(later - 1 - earlier, 0).astype(jnp.float32) * float(block_len)
    carry = jnp.where((earlier < later)[None], jnp.exp(-decays[:, None, None] * gap[None]), 0.0)
    state = jnp.einsum("mab,mbc->mac", carry, local_state, precision=HIGHEST)

    inter = jnp.einsum("rm,mbc->brc", left, state, precision=HIGHEST)
    return (intra + inter).reshape(positions, channels).astype(jnp.bfloat16)


def shards(proj, conv_weight, residues, decays, doc_lengths):
    kernel_len = conv_weight.shape[1]
    rows = proj.shape[0]
    ctx_size = lax.axis_size("ctx")
    mp_size = lax.axis_size("mp")
    lin_axis = ("ctx", "mp")
    tail_rows = shifted(proj[rows - (kernel_len - 1) :], lin_axis, 1)
    lin_index = lax.axis_index("ctx") * mp_size + lax.axis_index("mp")
    padded_pos = lin_index * rows - (kernel_len - 1) + jnp.arange(rows + kernel_len - 1, dtype=jnp.int32)
    padded_document_ids = document_number_index(doc_lengths, padded_pos)
    padded = jnp.concatenate([tail_rows, proj], axis=0)
    conv = short_convolution(padded, conv_weight, padded_document_ids, padded_pos, rows)
    query_part = conv[:, 0]
    product = (conv[:, 1] * conv[:, 2]).astype(jnp.bfloat16)

    swap_axis = ("mp", "ctx")
    gathered = lax.all_to_all(product, swap_axis, split_axis=1, concat_axis=0, tiled=True)
    width = gathered.shape[1]
    gathered = gathered.reshape(mp_size, ctx_size, rows, width).transpose(1, 0, 2, 3)
    gathered = gathered.reshape(ctx_size * mp_size * rows, width)
    groups_here = residues.shape[0]
    group_span = proj.shape[2] // mp_size // groups_here
    local_group = lax.axis_index("ctx") * width // group_span
    coefficient = residues[local_group] * jnp.sqrt(decays[local_group])
    filtered = long_filter(gathered, coefficient, decays[local_group], 256)
    filtered = filtered.reshape(ctx_size, mp_size, rows, width).transpose(1, 0, 2, 3)
    filtered = filtered.reshape(ctx_size * mp_size * rows, width)
    filtered = lax.all_to_all(filtered, swap_axis, split_axis=0, concat_axis=1, tiled=True)
    return (query_part * filtered.astype(jnp.float32)).astype(jnp.bfloat16)


def solution(mesh):
    return jax.shard_map(
        shards,
        mesh=mesh,
        in_specs=(P(("ctx", "mp"), None, None), P(), P("mp", None), P("mp", None), P()),
        out_specs=P(("ctx", "mp"), None),
        check_vma=False,
    )
```

```python
import jax
import jax.numpy as jnp
from jax import lax
from jax.sharding import PartitionSpec as P

HIGHEST = lax.Precision.HIGHEST


def shifted(block, axis, distance):
    count = lax.axis_size(axis)
    route = [(i, i + distance) for i in range(count - distance)]
    return lax.ppermute(block, axis, route)


def document_number_index(doc_lengths, positions):
    doc_starts = jnp.cumsum(doc_lengths) - doc_lengths
    inside = (doc_starts[None, :] <= positions[:, None]).astype(jnp.int32)
    return jnp.sum(inside, axis=1) - 1


def short_convolution(padded, conv_weight, padded_document_ids, padded_pos, out_rows):
    kernel_len = conv_weight.shape[1]
    result = jnp.zeros((out_rows,) + padded.shape[1:], jnp.float32)
    own_docs = padded_document_ids[kernel_len - 1 :]
    for position_shift in range(kernel_len):
        begin_row = kernel_len - 1 - position_shift
        earlier = padded[begin_row : begin_row + out_rows].astype(jnp.float32)
        keep_mask = (padded_document_ids[begin_row : begin_row + out_rows] == own_docs) & (
            padded_pos[begin_row : begin_row + out_rows] >= 0
        )
        result = (
            result
            + conv_weight[:, position_shift, :][None]
            * earlier
            * keep_mask.astype(jnp.float32)[:, None, None]
        )
    return result


def split_product(form, weights, inputs):
    upper_part = weights.astype(jnp.bfloat16)
    lower_part = (weights - upper_part.astype(jnp.float32)).astype(jnp.bfloat16)
    first = jnp.einsum(form, upper_part, inputs, preferred_element_type=jnp.float32)
    return first + jnp.einsum(form, lower_part, inputs, preferred_element_type=jnp.float32)


def long_filter(product, residues, decays):
    block_len, channels = product.shape
    group_count = residues.shape[0]
    group_width = channels // group_count
    coefficient = residues * jnp.sqrt(decays)
    offsets = jnp.arange(block_len, dtype=jnp.float32)
    left = coefficient[:, None, :] * jnp.exp(-decays[:, None, :] * offsets[None, :, None])
    right = jnp.exp(decays[:, :, None] * offsets[None, None, :])
    tile = jnp.einsum("grm,gms->grs", left, right, precision=HIGHEST)
    lag = jnp.arange(block_len)[:, None] - jnp.arange(block_len)[None, :]
    tile = jnp.where((lag >= 0)[None], tile, 0.0)
    inputs = product.reshape(block_len, group_count, group_width)
    intra = split_product("grs,sgc->rgc", tile, inputs)

    end_weight = jnp.exp(-decays[:, :, None] * (float(block_len) - offsets)[None, None, :])
    local_state = split_product("gms,sgc->gmc", end_weight, inputs)

    count = lax.axis_size("ctx")
    radix = min(4, count)

    def decay_of(distance):
        return jnp.exp(-decays * float(block_len * distance))[:, :, None]

    window = shifted(local_state, "ctx", 1)
    for distance in range(2, radix + 1):
        window = window + decay_of(distance - 1) * shifted(local_state, "ctx", distance)
    state = window
    for distance in range(radix, count, radix):
        state = state + decay_of(distance) * shifted(window, "ctx", distance)

    inter = jnp.einsum("grm,gmc->rgc", left, state, precision=HIGHEST)
    return (intra + inter).reshape(block_len, channels).astype(jnp.bfloat16)


def shards(proj, conv_weight, residues, decays, doc_lengths):
    kernel_len = conv_weight.shape[1]
    rows = proj.shape[0]
    lin_axis = ("ctx", "mp")
    tail_rows = shifted(proj[rows - (kernel_len - 1) :], lin_axis, 1)
    lin_index = lax.axis_index("ctx") * lax.axis_size("mp") + lax.axis_index("mp")
    padded_pos = lin_index * rows - (kernel_len - 1) + jnp.arange(rows + kernel_len - 1, dtype=jnp.int32)
    padded_document_ids = document_number_index(doc_lengths, padded_pos)
    padded = jnp.concatenate([tail_rows, proj], axis=0)
    conv = short_convolution(padded, conv_weight, padded_document_ids, padded_pos, rows)
    query_part = conv[:, 0]
    product = (conv[:, 1] * conv[:, 2]).astype(jnp.bfloat16)
    channel_rows = lax.all_to_all(product, "mp", split_axis=1, concat_axis=0, tiled=True)
    filtered = long_filter(channel_rows, residues, decays)
    filtered = lax.all_to_all(filtered, "mp", split_axis=0, concat_axis=1, tiled=True)
    return (query_part * filtered.astype(jnp.float32)).astype(jnp.bfloat16)


def solution(mesh):
    return jax.shard_map(
        shards,
        mesh=mesh,
        in_specs=(P(("ctx", "mp"), None, None), P(), P("mp", None), P("mp", None), P()),
        out_specs=P(("ctx", "mp"), None),
        check_vma=False,
    )
```

```python
import jax
import jax.numpy as jnp
from jax import lax
from jax.sharding import PartitionSpec as P

HIGHEST = lax.Precision.HIGHEST


def shifted(block, axis, distance):
    count = lax.axis_size(axis)
    route = [(i, i + distance) for i in range(count - distance)]
    return lax.ppermute(block, axis, route)


def document_number_index(doc_lengths, positions):
    doc_starts = jnp.cumsum(doc_lengths) - doc_lengths
    inside = (doc_starts[None, :] <= positions[:, None]).astype(jnp.int32)
    return jnp.sum(inside, axis=1) - 1


def short_convolution(padded, conv_weight, padded_document_ids, padded_pos, out_rows):
    kernel_len = conv_weight.shape[1]
    result = jnp.zeros((out_rows,) + padded.shape[1:], jnp.float32)
    own_docs = padded_document_ids[kernel_len - 1 :]
    for position_shift in range(kernel_len):
        begin_row = kernel_len - 1 - position_shift
        earlier = padded[begin_row : begin_row + out_rows].astype(jnp.float32)
        keep_mask = (padded_document_ids[begin_row : begin_row + out_rows] == own_docs) & (
            padded_pos[begin_row : begin_row + out_rows] >= 0
        )
        result = (
            result
            + conv_weight[:, position_shift, :][None]
            * earlier
            * keep_mask.astype(jnp.float32)[:, None, None]
        )
    return result


def split_product(form, weights, inputs):
    upper_part = weights.astype(jnp.bfloat16)
    lower_part = (weights - upper_part.astype(jnp.float32)).astype(jnp.bfloat16)
    first = jnp.einsum(form, upper_part, inputs, preferred_element_type=jnp.float32)
    return first + jnp.einsum(form, lower_part, inputs, preferred_element_type=jnp.float32)


def long_filter(product, residues, decays):
    block_len, channels = product.shape
    group_count = residues.shape[0]
    group_width = channels // group_count
    coefficient = residues * jnp.sqrt(decays)
    offsets = jnp.arange(block_len, dtype=jnp.float32)
    left = coefficient[:, None, :] * jnp.exp(-decays[:, None, :] * offsets[None, :, None])
    right = jnp.exp(decays[:, :, None] * offsets[None, None, :])
    tile = jnp.einsum("grm,gms->grs", left, right, precision=HIGHEST)
    lag = jnp.arange(block_len)[:, None] - jnp.arange(block_len)[None, :]
    tile = jnp.where((lag >= 0)[None], tile, 0.0)
    inputs = product.reshape(block_len, group_count, group_width)
    intra = split_product("grs,sgc->rgc", tile, inputs)

    end_weight = jnp.exp(-decays[:, :, None] * (float(block_len) - offsets)[None, None, :])
    local_state = split_product("gms,sgc->gmc", end_weight, inputs)

    count = lax.axis_size("ctx")
    flat = local_state.reshape(1, -1)
    sent = jnp.broadcast_to(flat, (count, flat.shape[1]))
    gathered = lax.all_to_all(sent, "ctx", split_axis=0, concat_axis=0, tiled=True)
    gathered = gathered.reshape((count,) + local_state.shape)
    here = lax.axis_index("ctx")
    earlier = jnp.arange(count, dtype=jnp.int32)
    gap = (here - 1 - earlier).astype(jnp.float32) * float(block_len)
    weight = jnp.where(
        (earlier < here)[:, None, None],
        jnp.exp(-decays[None] * jnp.maximum(gap, 0.0)[:, None, None]),
        0.0,
    )
    state = jnp.sum(weight[:, :, :, None] * gathered, axis=0)

    inter = jnp.einsum("grm,gmc->rgc", left, state, precision=HIGHEST)
    return (intra + inter).reshape(block_len, channels).astype(jnp.bfloat16)


def shards(proj, conv_weight, residues, decays, doc_lengths):
    kernel_len = conv_weight.shape[1]
    rows = proj.shape[0]
    lin_axis = ("ctx", "mp")
    tail_rows = shifted(proj[rows - (kernel_len - 1) :], lin_axis, 1)
    lin_index = lax.axis_index("ctx") * lax.axis_size("mp") + lax.axis_index("mp")
    padded_pos = lin_index * rows - (kernel_len - 1) + jnp.arange(rows + kernel_len - 1, dtype=jnp.int32)
    padded_document_ids = document_number_index(doc_lengths, padded_pos)
    padded = jnp.concatenate([tail_rows, proj], axis=0)
    conv = short_convolution(padded, conv_weight, padded_document_ids, padded_pos, rows)
    query_part = conv[:, 0]
    product = (conv[:, 1] * conv[:, 2]).astype(jnp.bfloat16)
    channel_rows = lax.all_to_all(product, "mp", split_axis=1, concat_axis=0, tiled=True)
    filtered = long_filter(channel_rows, residues, decays)
    filtered = lax.all_to_all(filtered, "mp", split_axis=0, concat_axis=1, tiled=True)
    return (query_part * filtered.astype(jnp.float32)).astype(jnp.bfloat16)


def solution(mesh):
    return jax.shard_map(
        shards,
        mesh=mesh,
        in_specs=(P(("ctx", "mp"), None, None), P(), P("mp", None), P("mp", None), P()),
        out_specs=P(("ctx", "mp"), None),
        check_vma=False,
    )
```

```python
import jax
import jax.numpy as jnp
from jax import lax
from jax.sharding import Mesh, NamedSharding, PartitionSpec as P

HIGHEST = lax.Precision.HIGHEST


def shifted(block, axis, distance):
    count = lax.axis_size(axis)
    route = [(i, i + distance) for i in range(count - distance)]
    return lax.ppermute(block, axis, route)


def document_number_index(doc_lengths, positions):
    doc_starts = jnp.cumsum(doc_lengths) - doc_lengths
    inside = (doc_starts[None, :] <= positions[:, None]).astype(jnp.int32)
    return jnp.sum(inside, axis=1) - 1


def short_convolution(padded, conv_weight, padded_document_ids, padded_pos, out_rows):
    kernel_len = conv_weight.shape[1]
    result = jnp.zeros((out_rows,) + padded.shape[1:], jnp.float32)
    own_docs = padded_document_ids[kernel_len - 1 :]
    for position_shift in range(kernel_len):
        begin_row = kernel_len - 1 - position_shift
        earlier = padded[begin_row : begin_row + out_rows].astype(jnp.float32)
        keep_mask = (padded_document_ids[begin_row : begin_row + out_rows] == own_docs) & (
            padded_pos[begin_row : begin_row + out_rows] >= 0
        )
        result = (
            result
            + conv_weight[:, position_shift, :][None]
            * earlier
            * keep_mask.astype(jnp.float32)[:, None, None]
        )
    return result


def split_product(form, weights, inputs):
    upper_part = weights.astype(jnp.bfloat16)
    lower_part = (weights - upper_part.astype(jnp.float32)).astype(jnp.bfloat16)
    first = jnp.einsum(form, upper_part, inputs, preferred_element_type=jnp.float32)
    return first + jnp.einsum(form, lower_part, inputs, preferred_element_type=jnp.float32)


def long_filter(product, residues, decays, block_len, outer_axis):
    positions, channels = product.shape
    group_count = residues.shape[0]
    group_width = channels // group_count
    block_count = positions // block_len
    coefficient = residues * jnp.sqrt(decays)
    offsets = jnp.arange(block_len, dtype=jnp.float32)
    left = coefficient[:, None, :] * jnp.exp(-decays[:, None, :] * offsets[None, :, None])
    right = jnp.exp(decays[:, :, None] * offsets[None, None, :])
    tile = jnp.einsum("grm,gms->grs", left, right, precision=HIGHEST)
    lag = jnp.arange(block_len)[:, None] - jnp.arange(block_len)[None, :]
    tile = jnp.where((lag >= 0)[None], tile, 0.0)
    inputs = product.reshape(block_count, block_len, group_count, group_width)
    intra = split_product("grs,bsgc->brgc", tile, inputs)

    end_weight = jnp.exp(-decays[:, :, None] * (float(block_len) - offsets)[None, None, :])
    block_state = split_product("gms,bsgc->gmbc", end_weight, inputs)

    blocks = jnp.arange(block_count, dtype=jnp.float32)
    to_end = jnp.exp(-decays[:, :, None] * (float(block_len) * (block_count - 1 - blocks))[None, None, :])
    run_state = jnp.einsum("gmb,gmbc->gmc", to_end, block_state, precision=HIGHEST)
    count = lax.axis_size(outer_axis)
    flat = run_state.reshape(1, -1)
    sent = jnp.broadcast_to(flat, (count, flat.shape[1]))
    gathered = lax.all_to_all(sent, outer_axis, split_axis=0, concat_axis=0, tiled=True)
    gathered = gathered.reshape((count,) + run_state.shape)
    here = lax.axis_index(outer_axis)
    earlier = jnp.arange(count, dtype=jnp.int32)
    gap = (here - 1 - earlier).astype(jnp.float32) * float(positions)
    weight = jnp.where(
        (earlier < here)[:, None, None],
        jnp.exp(-decays[None] * jnp.maximum(gap, 0.0)[:, None, None]),
        0.0,
    )
    incoming = jnp.sum(weight[:, :, :, None] * gathered, axis=0)

    later = jnp.arange(block_count)[:, None]
    before = jnp.arange(block_count)[None, :]
    block_gap = jnp.maximum(later - 1 - before, 0).astype(jnp.float32) * float(block_len)
    carry = jnp.where((before < later)[None, None], jnp.exp(-decays[:, :, None, None] * block_gap[None, None]), 0.0)
    start_decay = jnp.exp(-decays[:, :, None] * (float(block_len) * blocks)[None, None, :])
    state = jnp.einsum("gmab,gmbc->gmac", carry, block_state, precision=HIGHEST)
    state = state + start_decay[:, :, :, None] * incoming[:, :, None, :]

    inter = jnp.einsum("grm,gmbc->brgc", left, state, precision=HIGHEST)
    return (intra + inter).reshape(positions, channels).astype(jnp.bfloat16)


def shards(proj, conv_weight, residues, decays, doc_lengths):
    kernel_len = conv_weight.shape[1]
    rows = proj.shape[0]
    outer_size = lax.axis_size("zo")
    inner_size = lax.axis_size("zi")
    mp_size = lax.axis_size("mp")
    lin_axis = ("zo", "zi", "mp")
    tail_rows = shifted(proj[rows - (kernel_len - 1) :], lin_axis, 1)
    lin_index = (lax.axis_index("zo") * inner_size + lax.axis_index("zi")) * mp_size + lax.axis_index("mp")
    padded_pos = lin_index * rows - (kernel_len - 1) + jnp.arange(rows + kernel_len - 1, dtype=jnp.int32)
    padded_document_ids = document_number_index(doc_lengths, padded_pos)
    padded = jnp.concatenate([tail_rows, proj], axis=0)
    conv = short_convolution(padded, conv_weight, padded_document_ids, padded_pos, rows)
    query_part = conv[:, 0]
    product = (conv[:, 1] * conv[:, 2]).astype(jnp.bfloat16)

    swap_axis = ("mp", "zi")
    gathered = lax.all_to_all(product, swap_axis, split_axis=1, concat_axis=0, tiled=True)
    width = gathered.shape[1]
    gathered = gathered.reshape(mp_size, inner_size, rows, width).transpose(1, 0, 2, 3)
    gathered = gathered.reshape(inner_size * mp_size * rows, width)
    groups_here = residues.shape[0] // inner_size
    first_group = lax.axis_index("zi") * groups_here
    local_residues = lax.dynamic_slice_in_dim(residues, first_group, groups_here, 0)
    local_decays = lax.dynamic_slice_in_dim(decays, first_group, groups_here, 0)
    block_len = min(256, gathered.shape[0])
    filtered = long_filter(gathered, local_residues, local_decays, block_len, "zo")
    filtered = filtered.reshape(inner_size, mp_size, rows, width).transpose(1, 0, 2, 3)
    filtered = filtered.reshape(inner_size * mp_size * rows, width)
    filtered = lax.all_to_all(filtered, swap_axis, split_axis=0, concat_axis=1, tiled=True)
    return (query_part * filtered.astype(jnp.float32)).astype(jnp.bfloat16)


def solution(mesh):
    ctx_size, mp_size = mesh.devices.shape
    inner = 4 if ctx_size % 4 == 0 else 1
    split_mesh = Mesh(mesh.devices.reshape(ctx_size // inner, inner, mp_size), ("zo", "zi", "mp"))
    mapped = jax.shard_map(
        shards,
        mesh=split_mesh,
        in_specs=(P(("zo", "zi", "mp"), None, None), P(), P("mp", None), P("mp", None), P()),
        out_specs=P(("zo", "zi", "mp"), None),
        check_vma=False,
    )
    placed = NamedSharding(mesh, P(("ctx", "mp"), None))

    def run(*args):
        return lax.with_sharding_constraint(mapped(*args), placed)

    return run
```

```python
import jax
import jax.numpy as jnp
from jax import lax
from jax.sharding import Mesh, NamedSharding, PartitionSpec as P

HIGHEST = lax.Precision.HIGHEST


def shifted(block, axis, distance):
    count = lax.axis_size(axis)
    route = [(i, i + distance) for i in range(count - distance)]
    return lax.ppermute(block, axis, route)


def document_number_index(doc_lengths, positions):
    doc_starts = jnp.cumsum(doc_lengths) - doc_lengths
    inside = (doc_starts[None, :] <= positions[:, None]).astype(jnp.int32)
    return jnp.sum(inside, axis=1) - 1


def short_convolution(padded, weight_rows, keep, out_rows, feature, kernel_len):
    result = None
    for position_shift in range(kernel_len):
        begin_row = kernel_len - 1 - position_shift
        earlier = padded[begin_row : begin_row + out_rows, feature].astype(jnp.float32)
        tap = weight_rows[feature * kernel_len + position_shift][None, :]
        term = (tap * earlier) * keep[:, position_shift : position_shift + 1]
        result = term if result is None else result + term
    return result


def split_product(form, weights, inputs):
    upper_part = weights.astype(jnp.bfloat16)
    lower_part = (weights - upper_part.astype(jnp.float32)).astype(jnp.bfloat16)
    first = jnp.einsum(form, upper_part, inputs, preferred_element_type=jnp.float32)
    return first + jnp.einsum(form, lower_part, inputs, preferred_element_type=jnp.float32)


def long_filter(product, residues, decays, block_len, outer_axis):
    positions, channels = product.shape
    group_count = residues.shape[0]
    group_width = channels // group_count
    block_count = positions // block_len
    coefficient = residues * jnp.sqrt(decays)
    offsets = jnp.arange(block_len, dtype=jnp.float32)
    left = coefficient[:, None, :] * jnp.exp(-decays[:, None, :] * offsets[None, :, None])
    right = jnp.exp(decays[:, :, None] * offsets[None, None, :])
    tile = jnp.einsum("grm,gms->grs", left, right, precision=HIGHEST)
    lag = jnp.arange(block_len)[:, None] - jnp.arange(block_len)[None, :]
    tile = jnp.where((lag >= 0)[None], tile, 0.0)
    inputs = product.reshape(block_count, block_len, group_count, group_width)
    intra = split_product("grs,bsgc->brgc", tile, inputs)

    end_weight = jnp.exp(-decays[:, :, None] * (float(block_len) - offsets)[None, None, :])
    block_state = split_product("gms,bsgc->gmbc", end_weight, inputs)

    blocks = jnp.arange(block_count, dtype=jnp.float32)
    to_end = jnp.exp(-decays[:, :, None] * (float(block_len) * (block_count - 1 - blocks))[None, None, :])
    run_state = jnp.einsum("gmb,gmbc->gmc", to_end, block_state, precision=HIGHEST)
    count = lax.axis_size(outer_axis)
    flat = run_state.reshape(1, -1)
    sent = jnp.broadcast_to(flat, (count, flat.shape[1]))
    gathered = lax.all_to_all(sent, outer_axis, split_axis=0, concat_axis=0, tiled=True)
    gathered = gathered.reshape((count,) + run_state.shape)
    here = lax.axis_index(outer_axis)
    earlier = jnp.arange(count, dtype=jnp.int32)
    gap = (here - 1 - earlier).astype(jnp.float32) * float(positions)
    weight = jnp.where(
        (earlier < here)[:, None, None],
        jnp.exp(-decays[None] * jnp.maximum(gap, 0.0)[:, None, None]),
        0.0,
    )
    incoming = jnp.sum(weight[:, :, :, None] * gathered, axis=0)

    later = jnp.arange(block_count)[:, None]
    before = jnp.arange(block_count)[None, :]
    block_gap = jnp.maximum(later - 1 - before, 0).astype(jnp.float32) * float(block_len)
    carry = jnp.where((before < later)[None, None], jnp.exp(-decays[:, :, None, None] * block_gap[None, None]), 0.0)
    start_decay = jnp.exp(-decays[:, :, None] * (float(block_len) * blocks)[None, None, :])
    state = jnp.einsum("gmab,gmbc->gmac", carry, block_state, precision=HIGHEST)
    state = state + start_decay[:, :, :, None] * incoming[:, :, None, :]

    inter = jnp.einsum("grm,gmbc->brgc", left, state, precision=HIGHEST)
    return (intra + inter).reshape(positions, channels).astype(jnp.bfloat16)


def shards(proj, conv_weight, residues, decays, doc_lengths):
    kernel_len = conv_weight.shape[1]
    rows = proj.shape[0]
    outer_size = lax.axis_size("zo")
    inner_size = lax.axis_size("zi")
    mp_size = lax.axis_size("mp")
    lin_axis = ("zo", "zi", "mp")
    tail_rows = shifted(proj[rows - (kernel_len - 1) :], lin_axis, 1)
    lin_index = (lax.axis_index("zo") * inner_size + lax.axis_index("zi")) * mp_size + lax.axis_index("mp")
    padded_pos = lin_index * rows - (kernel_len - 1) + jnp.arange(rows + kernel_len - 1, dtype=jnp.int32)
    padded_document_ids = document_number_index(doc_lengths, padded_pos)
    padded = jnp.concatenate([tail_rows, proj], axis=0)
    own_docs = padded_document_ids[kernel_len - 1 :]
    keep = jnp.stack(
        [
            (padded_document_ids[kernel_len - 1 - k : kernel_len - 1 - k + rows] == own_docs)
            & (padded_pos[kernel_len - 1 - k : kernel_len - 1 - k + rows] >= 0)
            for k in range(kernel_len)
        ],
        axis=1,
    ).astype(jnp.float32)
    weight_rows = conv_weight.reshape(-1, conv_weight.shape[2])
    query_part = short_convolution(padded, weight_rows, keep, rows, 0, kernel_len)
    keys = short_convolution(padded, weight_rows, keep, rows, 1, kernel_len)
    values = short_convolution(padded, weight_rows, keep, rows, 2, kernel_len)
    product = (keys * values).astype(jnp.bfloat16)

    swap_axis = ("mp", "zi")
    gathered = lax.all_to_all(product, swap_axis, split_axis=1, concat_axis=0, tiled=True)
    width = gathered.shape[1]
    gathered = gathered.reshape(mp_size, inner_size, rows, width).transpose(1, 0, 2, 3)
    gathered = gathered.reshape(inner_size * mp_size * rows, width)
    groups_here = residues.shape[0] // inner_size
    first_group = lax.axis_index("zi") * groups_here
    local_residues = lax.dynamic_slice_in_dim(residues, first_group, groups_here, 0)
    local_decays = lax.dynamic_slice_in_dim(decays, first_group, groups_here, 0)
    block_len = min(256, gathered.shape[0])
    filtered = long_filter(gathered, local_residues, local_decays, block_len, "zo")
    filtered = filtered.reshape(inner_size, mp_size, rows, width).transpose(1, 0, 2, 3)
    filtered = filtered.reshape(inner_size * mp_size * rows, width)
    filtered = lax.all_to_all(filtered, swap_axis, split_axis=0, concat_axis=1, tiled=True)
    return (query_part * filtered.astype(jnp.float32)).astype(jnp.bfloat16)


def solution(mesh):
    ctx_size, mp_size = mesh.devices.shape
    inner = 4 if ctx_size % 4 == 0 else 1
    split_mesh = Mesh(mesh.devices.reshape(ctx_size // inner, inner, mp_size), ("zo", "zi", "mp"))
    mapped = jax.shard_map(
        shards,
        mesh=split_mesh,
        in_specs=(P(("zo", "zi", "mp"), None, None), P(), P("mp", None), P("mp", None), P()),
        out_specs=P(("zo", "zi", "mp"), None),
        check_vma=False,
    )
    placed = NamedSharding(mesh, P(("ctx", "mp"), None))

    def run(*args):
        return lax.with_sharding_constraint(mapped(*args), placed)

    return run
```

```python
import jax
import jax.numpy as jnp
from jax import lax
from jax.experimental import pallas as pl
from jax.experimental.pallas import tpu as pltpu
from jax.sharding import Mesh, NamedSharding, PartitionSpec as P

HIGHEST = lax.Precision.HIGHEST


def shifted(block, axis, distance):
    count = lax.axis_size(axis)
    route = [(i, i + distance) for i in range(count - distance)]
    return lax.ppermute(block, axis, route)


def document_number_index(doc_lengths, positions):
    doc_starts = jnp.cumsum(doc_lengths) - doc_lengths
    inside = (doc_starts[None, :] <= positions[:, None]).astype(jnp.int32)
    return jnp.sum(inside, axis=1) - 1


def conv_kernel(x_ref, w_ref, keep_ref, q_ref, u_ref, scratch):
    kernel_len = w_ref.shape[1]
    out_rows = q_ref.shape[0]
    keep = keep_ref[...]
    results = []
    for feature in range(x_ref.shape[0]):
        scratch[0 : out_rows + kernel_len - 1, :] = x_ref[feature].astype(jnp.float32)
        weights = w_ref[feature]
        total = None
        for position_shift in range(kernel_len):
            begin_row = kernel_len - 1 - position_shift
            earlier = scratch[begin_row : begin_row + out_rows, :]
            term = earlier * weights[position_shift : position_shift + 1, :] * keep[:, position_shift : position_shift + 1]
            total = term if total is None else total + term
        results.append(total)
    q_ref[...] = results[0]
    u_ref[...] = (results[1] * results[2]).astype(u_ref.dtype)


def short_convolution(padded, conv_weight, keep, out_rows):
    features, padded_rows, channels = padded.shape
    kernel_len = conv_weight.shape[1]
    tile = 1024 if channels % 1024 == 0 else channels
    return pl.pallas_call(
        conv_kernel,
        grid=(channels // tile,),
        in_specs=[
            pl.BlockSpec((features, padded_rows, tile), lambda j: (0, 0, j)),
            pl.BlockSpec((features, kernel_len, tile), lambda j: (0, 0, j)),
            pl.BlockSpec(keep.shape, lambda j: (0, 0)),
        ],
        out_specs=[
            pl.BlockSpec((out_rows, tile), lambda j: (0, j)),
            pl.BlockSpec((out_rows, tile), lambda j: (0, j)),
        ],
        out_shape=[
            jax.ShapeDtypeStruct((out_rows, channels), jnp.float32),
            jax.ShapeDtypeStruct((out_rows, channels), jnp.bfloat16),
        ],
        scratch_shapes=[pltpu.VMEM((padded_rows + 8 - padded_rows % 8, tile), jnp.float32)],
    )(padded, conv_weight, keep)


def split_product(form, weights, inputs):
    upper_part = weights.astype(jnp.bfloat16)
    lower_part = (weights - upper_part.astype(jnp.float32)).astype(jnp.bfloat16)
    first = jnp.einsum(form, upper_part, inputs, preferred_element_type=jnp.float32)
    return first + jnp.einsum(form, lower_part, inputs, preferred_element_type=jnp.float32)


def long_filter(product, residues, decays, block_len, outer_axis):
    positions, channels = product.shape
    group_count = residues.shape[0]
    group_width = channels // group_count
    block_count = positions // block_len
    coefficient = residues * jnp.sqrt(decays)
    offsets = jnp.arange(block_len, dtype=jnp.float32)
    left = coefficient[:, None, :] * jnp.exp(-decays[:, None, :] * offsets[None, :, None])
    right = jnp.exp(decays[:, :, None] * offsets[None, None, :])
    tile = jnp.einsum("grm,gms->grs", left, right, precision=HIGHEST)
    lag = jnp.arange(block_len)[:, None] - jnp.arange(block_len)[None, :]
    tile = jnp.where((lag >= 0)[None], tile, 0.0)
    inputs = product.reshape(block_count, block_len, group_count, group_width)
    intra = split_product("grs,bsgc->brgc", tile, inputs)

    end_weight = jnp.exp(-decays[:, :, None] * (float(block_len) - offsets)[None, None, :])
    block_state = split_product("gms,bsgc->gmbc", end_weight, inputs)

    blocks = jnp.arange(block_count, dtype=jnp.float32)
    to_end = jnp.exp(-decays[:, :, None] * (float(block_len) * (block_count - 1 - blocks))[None, None, :])
    run_state = jnp.einsum("gmb,gmbc->gmc", to_end, block_state, precision=HIGHEST)
    count = lax.axis_size(outer_axis)
    flat = run_state.reshape(1, -1)
    sent = jnp.broadcast_to(flat, (count, flat.shape[1]))
    gathered = lax.all_to_all(sent, outer_axis, split_axis=0, concat_axis=0, tiled=True)
    gathered = gathered.reshape((count,) + run_state.shape)
    here = lax.axis_index(outer_axis)
    earlier = jnp.arange(count, dtype=jnp.int32)
    gap = (here - 1 - earlier).astype(jnp.float32) * float(positions)
    weight = jnp.where(
        (earlier < here)[:, None, None],
        jnp.exp(-decays[None] * jnp.maximum(gap, 0.0)[:, None, None]),
        0.0,
    )
    incoming = jnp.sum(weight[:, :, :, None] * gathered, axis=0)

    later = jnp.arange(block_count)[:, None]
    before = jnp.arange(block_count)[None, :]
    block_gap = jnp.maximum(later - 1 - before, 0).astype(jnp.float32) * float(block_len)
    carry = jnp.where((before < later)[None, None], jnp.exp(-decays[:, :, None, None] * block_gap[None, None]), 0.0)
    start_decay = jnp.exp(-decays[:, :, None] * (float(block_len) * blocks)[None, None, :])
    state = jnp.einsum("gmab,gmbc->gmac", carry, block_state, precision=HIGHEST)
    state = state + start_decay[:, :, :, None] * incoming[:, :, None, :]

    inter = jnp.einsum("grm,gmbc->brgc", left, state, precision=HIGHEST)
    return (intra + inter).reshape(positions, channels).astype(jnp.bfloat16)


def shards(proj, conv_weight, residues, decays, doc_lengths):
    kernel_len = conv_weight.shape[1]
    rows = proj.shape[0]
    outer_size = lax.axis_size("zo")
    inner_size = lax.axis_size("zi")
    mp_size = lax.axis_size("mp")
    lin_axis = ("zo", "zi", "mp")
    tail_rows = shifted(proj[rows - (kernel_len - 1) :], lin_axis, 1)
    lin_index = (lax.axis_index("zo") * inner_size + lax.axis_index("zi")) * mp_size + lax.axis_index("mp")
    padded_pos = lin_index * rows - (kernel_len - 1) + jnp.arange(rows + kernel_len - 1, dtype=jnp.int32)
    padded_document_ids = document_number_index(doc_lengths, padded_pos)
    padded = jnp.concatenate([tail_rows, proj], axis=0).transpose(1, 0, 2)
    own_docs = padded_document_ids[kernel_len - 1 :]
    keep = jnp.stack(
        [
            (padded_document_ids[kernel_len - 1 - k : kernel_len - 1 - k + rows] == own_docs)
            & (padded_pos[kernel_len - 1 - k : kernel_len - 1 - k + rows] >= 0)
            for k in range(kernel_len)
        ]
        + [jnp.zeros((rows,), bool)] * (8 - kernel_len % 8),
        axis=1,
    ).astype(jnp.float32)
    query_part, product = short_convolution(padded, conv_weight, keep, rows)

    swap_axis = ("mp", "zi")
    gathered = lax.all_to_all(product, swap_axis, split_axis=1, concat_axis=0, tiled=True)
    width = gathered.shape[1]
    gathered = gathered.reshape(mp_size, inner_size, rows, width).transpose(1, 0, 2, 3)
    gathered = gathered.reshape(inner_size * mp_size * rows, width)
    groups_here = residues.shape[0] // inner_size
    first_group = lax.axis_index("zi") * groups_here
    local_residues = lax.dynamic_slice_in_dim(residues, first_group, groups_here, 0)
    local_decays = lax.dynamic_slice_in_dim(decays, first_group, groups_here, 0)
    block_len = min(256, gathered.shape[0])
    filtered = long_filter(gathered, local_residues, local_decays, block_len, "zo")
    filtered = filtered.reshape(inner_size, mp_size, rows, width).transpose(1, 0, 2, 3)
    filtered = filtered.reshape(inner_size * mp_size * rows, width)
    filtered = lax.all_to_all(filtered, swap_axis, split_axis=0, concat_axis=1, tiled=True)
    return (query_part * filtered.astype(jnp.float32)).astype(jnp.bfloat16)


def solution(mesh):
    ctx_size, mp_size = mesh.devices.shape
    inner = 4 if ctx_size % 4 == 0 else 1
    split_mesh = Mesh(mesh.devices.reshape(ctx_size // inner, inner, mp_size), ("zo", "zi", "mp"))
    mapped = jax.shard_map(
        shards,
        mesh=split_mesh,
        in_specs=(P(("zo", "zi", "mp"), None, None), P(), P("mp", None), P("mp", None), P()),
        out_specs=P(("zo", "zi", "mp"), None),
        check_vma=False,
    )
    placed = NamedSharding(mesh, P(("ctx", "mp"), None))

    def run(*args):
        return lax.with_sharding_constraint(mapped(*args), placed)

    return run
```

```python
import jax
import jax.numpy as jnp
from jax import lax
from jax.sharding import Mesh, NamedSharding, PartitionSpec as P

HIGHEST = lax.Precision.HIGHEST


def shifted(block, axis, distance):
    count = lax.axis_size(axis)
    route = [(i, i + distance) for i in range(count - distance)]
    return lax.ppermute(block, axis, route)


def document_number_index(doc_lengths, positions):
    doc_starts = jnp.cumsum(doc_lengths) - doc_lengths
    inside = (doc_starts[None, :] <= positions[:, None]).astype(jnp.int32)
    return jnp.sum(inside, axis=1) - 1


def short_convolution(padded, conv_weight, padded_document_ids, padded_pos, out_rows):
    kernel_len = conv_weight.shape[1]
    result = jnp.zeros((out_rows,) + padded.shape[1:], jnp.float32)
    own_docs = padded_document_ids[kernel_len - 1 :]
    for position_shift in range(kernel_len):
        begin_row = kernel_len - 1 - position_shift
        earlier = padded[begin_row : begin_row + out_rows].astype(jnp.float32)
        keep_mask = (padded_document_ids[begin_row : begin_row + out_rows] == own_docs) & (
            padded_pos[begin_row : begin_row + out_rows] >= 0
        )
        result = (
            result
            + conv_weight[:, position_shift, :][None]
            * earlier
            * keep_mask.astype(jnp.float32)[:, None, None]
        )
    return result


def split_product(form, weights, inputs):
    upper_part = weights.astype(jnp.bfloat16)
    lower_part = (weights - upper_part.astype(jnp.float32)).astype(jnp.bfloat16)
    first = jnp.einsum(form, upper_part, inputs, preferred_element_type=jnp.float32)
    return first + jnp.einsum(form, lower_part, inputs, preferred_element_type=jnp.float32)


def long_filter(product, residues, decays, block_len, outer_axis):
    positions, channels = product.shape
    group_count = residues.shape[0]
    group_width = channels // group_count
    block_count = positions // block_len
    coefficient = residues * jnp.sqrt(decays)
    offsets = jnp.arange(block_len, dtype=jnp.float32)
    left = coefficient[:, None, :] * jnp.exp(-decays[:, None, :] * offsets[None, :, None])
    right = jnp.exp(decays[:, :, None] * offsets[None, None, :])
    tile = jnp.einsum("grm,gms->grs", left, right, precision=HIGHEST)
    lag = jnp.arange(block_len)[:, None] - jnp.arange(block_len)[None, :]
    tile = jnp.where((lag >= 0)[None], tile, 0.0)
    inputs = product.reshape(block_count, block_len, group_count, group_width)
    intra = split_product("grs,bsgc->brgc", tile, inputs)

    end_weight = jnp.exp(-decays[:, :, None] * (float(block_len) - offsets)[None, None, :])
    block_state = split_product("gms,bsgc->gmbc", end_weight, inputs)

    blocks = jnp.arange(block_count, dtype=jnp.float32)
    to_end = jnp.exp(-decays[:, :, None] * (float(block_len) * (block_count - 1 - blocks))[None, None, :])
    run_state = jnp.einsum("gmb,gmbc->gmc", to_end, block_state, precision=HIGHEST)
    count = lax.axis_size(outer_axis)
    flat = run_state.reshape(1, -1)
    sent = jnp.broadcast_to(flat, (count, flat.shape[1]))
    gathered = lax.all_to_all(sent, outer_axis, split_axis=0, concat_axis=0, tiled=True)
    gathered = gathered.reshape((count,) + run_state.shape)
    here = lax.axis_index(outer_axis)
    earlier = jnp.arange(count, dtype=jnp.int32)
    gap = (here - 1 - earlier).astype(jnp.float32) * float(positions)
    weight = jnp.where(
        (earlier < here)[:, None, None],
        jnp.exp(-decays[None] * jnp.maximum(gap, 0.0)[:, None, None]),
        0.0,
    )
    incoming = jnp.sum(weight[:, :, :, None] * gathered, axis=0)

    later = jnp.arange(block_count)[:, None]
    before = jnp.arange(block_count)[None, :]
    block_gap = jnp.maximum(later - 1 - before, 0).astype(jnp.float32) * float(block_len)
    carry = jnp.where((before < later)[None, None], jnp.exp(-decays[:, :, None, None] * block_gap[None, None]), 0.0)
    start_decay = jnp.exp(-decays[:, :, None] * (float(block_len) * blocks)[None, None, :])
    state = jnp.einsum("gmab,gmbc->gmac", carry, block_state, precision=HIGHEST)
    state = state + start_decay[:, :, :, None] * incoming[:, :, None, :]

    inter = jnp.einsum("grm,gmbc->brgc", left, state, precision=HIGHEST)
    return (intra + inter).reshape(positions, channels).astype(jnp.bfloat16)


def shards(proj, conv_weight, residues, decays, doc_lengths):
    kernel_len = conv_weight.shape[1]
    rows = proj.shape[0]
    outer_size = lax.axis_size("zo")
    inner_size = lax.axis_size("zi")
    mp_size = lax.axis_size("mp")
    lin_axis = ("zo", "zi", "mp")
    tail_rows = shifted(proj[rows - (kernel_len - 1) :], lin_axis, 1)
    lin_index = (lax.axis_index("zo") * inner_size + lax.axis_index("zi")) * mp_size + lax.axis_index("mp")
    padded_pos = lin_index * rows - (kernel_len - 1) + jnp.arange(rows + kernel_len - 1, dtype=jnp.int32)
    padded_document_ids = document_number_index(doc_lengths, padded_pos)
    head_rows = kernel_len - 1
    body = short_convolution(
        proj, conv_weight, padded_document_ids[head_rows:], padded_pos[head_rows:], rows - head_rows
    )
    head_input = jnp.concatenate([tail_rows, proj[:head_rows]], axis=0)
    head = short_convolution(
        head_input, conv_weight, padded_document_ids[: 2 * head_rows], padded_pos[: 2 * head_rows], head_rows
    )
    conv = jnp.concatenate([head, body], axis=0)
    query_part = conv[:, 0]
    product = (conv[:, 1] * conv[:, 2]).astype(jnp.bfloat16)

    swap_axis = ("mp", "zi")
    gathered = lax.all_to_all(product, swap_axis, split_axis=1, concat_axis=0, tiled=True)
    width = gathered.shape[1]
    gathered = gathered.reshape(mp_size, inner_size, rows, width).transpose(1, 0, 2, 3)
    gathered = gathered.reshape(inner_size * mp_size * rows, width)
    groups_here = residues.shape[0] // inner_size
    first_group = lax.axis_index("zi") * groups_here
    local_residues = lax.dynamic_slice_in_dim(residues, first_group, groups_here, 0)
    local_decays = lax.dynamic_slice_in_dim(decays, first_group, groups_here, 0)
    block_len = min(256, gathered.shape[0])
    filtered = long_filter(gathered, local_residues, local_decays, block_len, "zo")
    filtered = filtered.reshape(inner_size, mp_size, rows, width).transpose(1, 0, 2, 3)
    filtered = filtered.reshape(inner_size * mp_size * rows, width)
    filtered = lax.all_to_all(filtered, swap_axis, split_axis=0, concat_axis=1, tiled=True)
    return (query_part * filtered.astype(jnp.float32)).astype(jnp.bfloat16)


def solution(mesh):
    ctx_size, mp_size = mesh.devices.shape
    inner = 4 if ctx_size % 4 == 0 else 1
    split_mesh = Mesh(mesh.devices.reshape(ctx_size // inner, inner, mp_size), ("zo", "zi", "mp"))
    mapped = jax.shard_map(
        shards,
        mesh=split_mesh,
        in_specs=(P(("zo", "zi", "mp"), None, None), P(), P("mp", None), P("mp", None), P()),
        out_specs=P(("zo", "zi", "mp"), None),
        check_vma=False,
    )
    placed = NamedSharding(mesh, P(("ctx", "mp"), None))

    def run(*args):
        return lax.with_sharding_constraint(mapped(*args), placed)

    return run
```

```python
import jax
import jax.numpy as jnp
from jax import lax
from jax.sharding import Mesh, NamedSharding, PartitionSpec as P

HIGHEST = lax.Precision.HIGHEST


def shifted(block, axis, distance):
    count = lax.axis_size(axis)
    route = [(i, i + distance) for i in range(count - distance)]
    return lax.ppermute(block, axis, route)


def document_number_index(doc_lengths, positions):
    doc_starts = jnp.cumsum(doc_lengths) - doc_lengths
    inside = (doc_starts[None, :] <= positions[:, None]).astype(jnp.int32)
    return jnp.sum(inside, axis=1) - 1


def short_convolution(padded, conv_weight, padded_document_ids, padded_pos, out_rows):
    kernel_len = conv_weight.shape[1]
    result = jnp.zeros((out_rows,) + padded.shape[1:], jnp.float32)
    own_docs = padded_document_ids[kernel_len - 1 :]
    for position_shift in range(kernel_len):
        begin_row = kernel_len - 1 - position_shift
        earlier = padded[begin_row : begin_row + out_rows].astype(jnp.float32)
        keep_mask = (padded_document_ids[begin_row : begin_row + out_rows] == own_docs) & (
            padded_pos[begin_row : begin_row + out_rows] >= 0
        )
        result = (
            result
            + conv_weight[:, position_shift, :][None]
            * earlier
            * keep_mask.astype(jnp.float32)[:, None, None]
        )
    return result


def split_product(form, weights, inputs):
    upper_part = weights.astype(jnp.bfloat16)
    lower_part = (weights - upper_part.astype(jnp.float32)).astype(jnp.bfloat16)
    first = jnp.einsum(form, upper_part, inputs, preferred_element_type=jnp.float32)
    return first + jnp.einsum(form, lower_part, inputs, preferred_element_type=jnp.float32)


def long_filter(product, residues, decays, block_len, outer_axis):
    positions, channels = product.shape
    group_count = residues.shape[0]
    group_width = channels // group_count
    block_count = positions // block_len
    coefficient = residues * jnp.sqrt(decays)
    offsets = jnp.arange(block_len, dtype=jnp.float32)
    left = coefficient[:, None, :] * jnp.exp(-decays[:, None, :] * offsets[None, :, None])
    right = jnp.exp(decays[:, :, None] * offsets[None, None, :])
    tile = jnp.einsum("grm,gms->grs", left, right, precision=HIGHEST)
    lag = jnp.arange(block_len)[:, None] - jnp.arange(block_len)[None, :]
    tile = jnp.where((lag >= 0)[None], tile, 0.0)
    inputs = product.reshape(block_count, block_len, group_count, group_width)
    intra = split_product("grs,bsgc->brgc", tile, inputs)

    end_weight = jnp.exp(-decays[:, :, None] * (float(block_len) - offsets)[None, None, :])
    block_state = split_product("gms,bsgc->gmbc", end_weight, inputs)

    blocks = jnp.arange(block_count, dtype=jnp.float32)
    to_end = jnp.exp(-decays[:, :, None] * (float(block_len) * (block_count - 1 - blocks))[None, None, :])
    run_state = jnp.einsum("gmb,gmbc->gmc", to_end, block_state, precision=HIGHEST)
    count = lax.axis_size(outer_axis)
    gathered = lax.all_gather(run_state, outer_axis, axis=0)
    here = lax.axis_index(outer_axis)
    earlier = jnp.arange(count, dtype=jnp.int32)
    gap = (here - 1 - earlier).astype(jnp.float32) * float(positions)
    weight = jnp.where(
        (earlier < here)[:, None, None],
        jnp.exp(-decays[None] * jnp.maximum(gap, 0.0)[:, None, None]),
        0.0,
    )
    incoming = jnp.sum(weight[:, :, :, None] * gathered, axis=0)

    later = jnp.arange(block_count)[:, None]
    before = jnp.arange(block_count)[None, :]
    block_gap = jnp.maximum(later - 1 - before, 0).astype(jnp.float32) * float(block_len)
    carry = jnp.where((before < later)[None, None], jnp.exp(-decays[:, :, None, None] * block_gap[None, None]), 0.0)
    start_decay = jnp.exp(-decays[:, :, None] * (float(block_len) * blocks)[None, None, :])
    state = jnp.einsum("gmab,gmbc->gmac", carry, block_state, precision=HIGHEST)
    state = state + start_decay[:, :, :, None] * incoming[:, :, None, :]

    inter = jnp.einsum("grm,gmbc->brgc", left, state, precision=HIGHEST)
    return (intra + inter).reshape(positions, channels).astype(jnp.bfloat16)


def shards(proj, conv_weight, residues, decays, doc_lengths):
    kernel_len = conv_weight.shape[1]
    rows = proj.shape[0]
    outer_size = lax.axis_size("zo")
    inner_size = lax.axis_size("zi")
    mp_size = lax.axis_size("mp")
    lin_axis = ("zo", "zi", "mp")
    tail_rows = shifted(proj[rows - (kernel_len - 1) :], lin_axis, 1)
    lin_index = (lax.axis_index("zo") * inner_size + lax.axis_index("zi")) * mp_size + lax.axis_index("mp")
    padded_pos = lin_index * rows - (kernel_len - 1) + jnp.arange(rows + kernel_len - 1, dtype=jnp.int32)
    padded_document_ids = document_number_index(doc_lengths, padded_pos)
    padded = jnp.concatenate([tail_rows, proj], axis=0)
    conv = short_convolution(padded, conv_weight, padded_document_ids, padded_pos, rows)
    query_part = conv[:, 0]
    product = (conv[:, 1] * conv[:, 2]).astype(jnp.bfloat16)

    swap_axis = ("mp", "zi")
    gathered = lax.all_to_all(product, swap_axis, split_axis=1, concat_axis=0, tiled=True)
    width = gathered.shape[1]
    gathered = gathered.reshape(mp_size, inner_size, rows, width).transpose(1, 0, 2, 3)
    gathered = gathered.reshape(inner_size * mp_size * rows, width)
    groups_here = residues.shape[0] // inner_size
    first_group = lax.axis_index("zi") * groups_here
    local_residues = lax.dynamic_slice_in_dim(residues, first_group, groups_here, 0)
    local_decays = lax.dynamic_slice_in_dim(decays, first_group, groups_here, 0)
    block_len = min(256, gathered.shape[0])
    filtered = long_filter(gathered, local_residues, local_decays, block_len, "zo")
    filtered = filtered.reshape(inner_size, mp_size, rows, width).transpose(1, 0, 2, 3)
    filtered = filtered.reshape(inner_size * mp_size * rows, width)
    filtered = lax.all_to_all(filtered, swap_axis, split_axis=0, concat_axis=1, tiled=True)
    return (query_part * filtered.astype(jnp.float32)).astype(jnp.bfloat16)


def solution(mesh):
    ctx_size, mp_size = mesh.devices.shape
    inner = 4 if ctx_size % 4 == 0 else 1
    split_mesh = Mesh(mesh.devices.reshape(ctx_size // inner, inner, mp_size), ("zo", "zi", "mp"))
    mapped = jax.shard_map(
        shards,
        mesh=split_mesh,
        in_specs=(P(("zo", "zi", "mp"), None, None), P(), P("mp", None), P("mp", None), P()),
        out_specs=P(("zo", "zi", "mp"), None),
        check_vma=False,
    )
    placed = NamedSharding(mesh, P(("ctx", "mp"), None))

    def run(*args):
        return lax.with_sharding_constraint(mapped(*args), placed)

    return run
```

```python
import jax
import jax.numpy as jnp
from jax import lax
from jax.sharding import Mesh, NamedSharding, PartitionSpec as P

HIGHEST = lax.Precision.HIGHEST


def shifted(block, axis, distance):
    count = lax.axis_size(axis)
    route = [(i, i + distance) for i in range(count - distance)]
    return lax.ppermute(block, axis, route)


def document_number_index(doc_lengths, positions):
    doc_starts = jnp.cumsum(doc_lengths) - doc_lengths
    inside = (doc_starts[None, :] <= positions[:, None]).astype(jnp.int32)
    return jnp.sum(inside, axis=1) - 1


def short_convolution(padded, conv_weight, padded_document_ids, padded_pos, out_rows):
    kernel_len = conv_weight.shape[1]
    result = jnp.zeros((out_rows,) + padded.shape[1:], jnp.float32)
    own_docs = padded_document_ids[kernel_len - 1 :]
    for position_shift in range(kernel_len):
        begin_row = kernel_len - 1 - position_shift
        earlier = padded[begin_row : begin_row + out_rows].astype(jnp.float32)
        keep_mask = (padded_document_ids[begin_row : begin_row + out_rows] == own_docs) & (
            padded_pos[begin_row : begin_row + out_rows] >= 0
        )
        result = (
            result
            + conv_weight[:, position_shift, :][None]
            * earlier
            * keep_mask.astype(jnp.float32)[:, None, None]
        )
    return result


def split_product(form, weights, inputs):
    upper_part = weights.astype(jnp.bfloat16)
    lower_part = (weights - upper_part.astype(jnp.float32)).astype(jnp.bfloat16)
    first = jnp.einsum(form, upper_part, inputs, preferred_element_type=jnp.float32)
    return first + jnp.einsum(form, lower_part, inputs, preferred_element_type=jnp.float32)


def long_filter(product, residues, decays, block_len, outer_axis):
    positions, channels = product.shape
    group_count = residues.shape[0]
    group_width = channels // group_count
    block_count = positions // block_len
    coefficient = residues * jnp.sqrt(decays)
    offsets = jnp.arange(block_len, dtype=jnp.float32)
    left = coefficient[:, None, :] * jnp.exp(-decays[:, None, :] * offsets[None, :, None])
    right = jnp.exp(decays[:, :, None] * offsets[None, None, :])
    tile = jnp.einsum("grm,gms->grs", left, right, precision=HIGHEST)
    lag = jnp.arange(block_len)[:, None] - jnp.arange(block_len)[None, :]
    tile = jnp.where((lag >= 0)[None], tile, 0.0)
    inputs = product.reshape(block_count, block_len, group_count, group_width)
    intra = split_product("grs,bsgc->brgc", tile, inputs)

    end_weight = jnp.exp(-decays[:, :, None] * (float(block_len) - offsets)[None, None, :])
    block_state = split_product("gms,bsgc->gmbc", end_weight, inputs)

    blocks = jnp.arange(block_count, dtype=jnp.float32)
    to_end = jnp.exp(-decays[:, :, None] * (float(block_len) * (block_count - 1 - blocks))[None, None, :])
    run_state = jnp.einsum("gmb,gmbc->gmc", to_end, block_state, precision=HIGHEST)
    count = lax.axis_size(outer_axis)
    flat = run_state.reshape(1, -1)
    sent = jnp.broadcast_to(flat, (count, flat.shape[1]))
    gathered = lax.all_to_all(sent, outer_axis, split_axis=0, concat_axis=0, tiled=True)
    gathered = gathered.reshape((count,) + run_state.shape)
    here = lax.axis_index(outer_axis)
    earlier = jnp.arange(count, dtype=jnp.int32)
    gap = (here - 1 - earlier).astype(jnp.float32) * float(positions)
    weight = jnp.where(
        (earlier < here)[:, None, None],
        jnp.exp(-decays[None] * jnp.maximum(gap, 0.0)[:, None, None]),
        0.0,
    )
    incoming = jnp.sum(weight[:, :, :, None] * gathered, axis=0)

    later = jnp.arange(block_count)[:, None]
    before = jnp.arange(block_count)[None, :]
    block_gap = jnp.maximum(later - 1 - before, 0).astype(jnp.float32) * float(block_len)
    carry = jnp.where((before < later)[None, None], jnp.exp(-decays[:, :, None, None] * block_gap[None, None]), 0.0)
    start_decay = jnp.exp(-decays[:, :, None] * (float(block_len) * blocks)[None, None, :])
    state = jnp.einsum("gmab,gmbc->gmac", carry, block_state, precision=HIGHEST)
    state = state + start_decay[:, :, :, None] * incoming[:, :, None, :]

    inter = jnp.einsum("grm,gmbc->brgc", left, state, precision=HIGHEST)
    return (intra + inter).reshape(positions, channels).astype(jnp.bfloat16)


def shards(proj, conv_weight, residues, decays, doc_lengths):
    kernel_len = conv_weight.shape[1]
    rows = proj.shape[0]
    outer_size = lax.axis_size("zo")
    inner_size = lax.axis_size("zi")
    mp_size = lax.axis_size("mp")
    lin_axis = ("zo", "zi", "mp")
    tail_rows = shifted(proj[rows - (kernel_len - 1) :], lin_axis, 1)
    lin_index = (lax.axis_index("zo") * inner_size + lax.axis_index("zi")) * mp_size + lax.axis_index("mp")
    padded_pos = lin_index * rows - (kernel_len - 1) + jnp.arange(rows + kernel_len - 1, dtype=jnp.int32)
    padded_document_ids = document_number_index(doc_lengths, padded_pos)
    padded = jnp.concatenate([tail_rows, proj], axis=0)
    pair = short_convolution(padded[:, 1:], conv_weight[1:], padded_document_ids, padded_pos, rows)
    product = (pair[:, 0] * pair[:, 1]).astype(jnp.bfloat16)

    swap_axis = ("mp", "zi")
    gathered = lax.all_to_all(product, swap_axis, split_axis=1, concat_axis=0, tiled=True)
    width = gathered.shape[1]
    gathered = gathered.reshape(mp_size, inner_size, rows, width).transpose(1, 0, 2, 3)
    gathered = gathered.reshape(inner_size * mp_size * rows, width)
    groups_here = residues.shape[0] // inner_size
    first_group = lax.axis_index("zi") * groups_here
    local_residues = lax.dynamic_slice_in_dim(residues, first_group, groups_here, 0)
    local_decays = lax.dynamic_slice_in_dim(decays, first_group, groups_here, 0)
    block_len = min(256, gathered.shape[0])
    filtered = long_filter(gathered, local_residues, local_decays, block_len, "zo")
    filtered = filtered.reshape(inner_size, mp_size, rows, width).transpose(1, 0, 2, 3)
    filtered = filtered.reshape(inner_size * mp_size * rows, width)
    filtered = lax.all_to_all(filtered, swap_axis, split_axis=0, concat_axis=1, tiled=True)
    query_part = short_convolution(padded[:, :1], conv_weight[:1], padded_document_ids, padded_pos, rows)[:, 0]
    return (query_part * filtered.astype(jnp.float32)).astype(jnp.bfloat16)


def solution(mesh):
    ctx_size, mp_size = mesh.devices.shape
    inner = 4 if ctx_size % 4 == 0 else 1
    split_mesh = Mesh(mesh.devices.reshape(ctx_size // inner, inner, mp_size), ("zo", "zi", "mp"))
    mapped = jax.shard_map(
        shards,
        mesh=split_mesh,
        in_specs=(P(("zo", "zi", "mp"), None, None), P(), P("mp", None), P("mp", None), P()),
        out_specs=P(("zo", "zi", "mp"), None),
        check_vma=False,
    )
    placed = NamedSharding(mesh, P(("ctx", "mp"), None))

    def run(*args):
        return lax.with_sharding_constraint(mapped(*args), placed)

    return run
```

```python
import jax
import jax.numpy as jnp
from jax import lax
from jax.sharding import Mesh, NamedSharding, PartitionSpec as P

HIGHEST = lax.Precision.HIGHEST


def shifted(block, axis, distance):
    count = lax.axis_size(axis)
    route = [(i, i + distance) for i in range(count - distance)]
    return lax.ppermute(block, axis, route)


def document_number_index(doc_lengths, positions):
    doc_starts = jnp.cumsum(doc_lengths) - doc_lengths
    inside = (doc_starts[None, :] <= positions[:, None]).astype(jnp.int32)
    return jnp.sum(inside, axis=1) - 1


def short_convolution(padded, conv_weight, padded_document_ids, padded_pos, out_rows):
    kernel_len = conv_weight.shape[1]
    result = jnp.zeros((out_rows,) + padded.shape[1:], jnp.float32)
    own_docs = padded_document_ids[kernel_len - 1 :]
    for position_shift in range(kernel_len):
        begin_row = kernel_len - 1 - position_shift
        earlier = padded[begin_row : begin_row + out_rows].astype(jnp.float32)
        keep_mask = (padded_document_ids[begin_row : begin_row + out_rows] == own_docs) & (
            padded_pos[begin_row : begin_row + out_rows] >= 0
        )
        result = (
            result
            + conv_weight[:, position_shift, :][None]
            * earlier
            * keep_mask.astype(jnp.float32)[:, None, None]
        )
    return result


def split_product(form, weights, inputs):
    upper_part = weights.astype(jnp.bfloat16)
    lower_part = (weights - upper_part.astype(jnp.float32)).astype(jnp.bfloat16)
    first = jnp.einsum(form, upper_part, inputs, preferred_element_type=jnp.float32)
    return first + jnp.einsum(form, lower_part, inputs, preferred_element_type=jnp.float32)


def long_filter(product, residues, decays, block_len, outer_axis):
    positions, channels = product.shape
    group_count = residues.shape[0]
    group_width = channels // group_count
    block_count = positions // block_len
    coefficient = residues * jnp.sqrt(decays)
    offsets = jnp.arange(block_len, dtype=jnp.float32)
    left = coefficient[:, None, :] * jnp.exp(-decays[:, None, :] * offsets[None, :, None])
    right = jnp.exp(decays[:, :, None] * offsets[None, None, :])
    tile = jnp.einsum("grm,gms->grs", left, right, precision=HIGHEST)
    lag = jnp.arange(block_len)[:, None] - jnp.arange(block_len)[None, :]
    tile = jnp.where((lag >= 0)[None], tile, 0.0)
    inputs = product.reshape(block_count, block_len, group_count, group_width)
    intra = split_product("grs,bsgc->brgc", tile, inputs)

    end_weight = jnp.exp(-decays[:, :, None] * (float(block_len) - offsets)[None, None, :])
    block_state = split_product("gms,bsgc->gmbc", end_weight, inputs)

    blocks = jnp.arange(block_count, dtype=jnp.float32)
    to_end = jnp.exp(-decays[:, :, None] * (float(block_len) * (block_count - 1 - blocks))[None, None, :])
    run_state = jnp.einsum("gmb,gmbc->gmc", to_end, block_state, precision=HIGHEST)
    count = lax.axis_size(outer_axis)
    incoming = shifted(run_state, outer_axis, 1)
    distance = 1
    while distance < count - 1:
        decay_k = jnp.exp(-decays * float(positions * distance))[:, :, None]
        incoming = incoming + decay_k * shifted(incoming, outer_axis, distance)
        distance *= 2

    later = jnp.arange(block_count)[:, None]
    before = jnp.arange(block_count)[None, :]
    block_gap = jnp.maximum(later - 1 - before, 0).astype(jnp.float32) * float(block_len)
    carry = jnp.where((before < later)[None, None], jnp.exp(-decays[:, :, None, None] * block_gap[None, None]), 0.0)
    start_decay = jnp.exp(-decays[:, :, None] * (float(block_len) * blocks)[None, None, :])
    state = jnp.einsum("gmab,gmbc->gmac", carry, block_state, precision=HIGHEST)
    state = state + start_decay[:, :, :, None] * incoming[:, :, None, :]

    inter = jnp.einsum("grm,gmbc->brgc", left, state, precision=HIGHEST)
    return (intra + inter).reshape(positions, channels).astype(jnp.bfloat16)


def shards(proj, conv_weight, residues, decays, doc_lengths):
    kernel_len = conv_weight.shape[1]
    rows = proj.shape[0]
    outer_size = lax.axis_size("zo")
    inner_size = lax.axis_size("zi")
    mp_size = lax.axis_size("mp")
    lin_axis = ("zo", "zi", "mp")
    tail_rows = shifted(proj[rows - (kernel_len - 1) :], lin_axis, 1)
    lin_index = (lax.axis_index("zo") * inner_size + lax.axis_index("zi")) * mp_size + lax.axis_index("mp")
    padded_pos = lin_index * rows - (kernel_len - 1) + jnp.arange(rows + kernel_len - 1, dtype=jnp.int32)
    padded_document_ids = document_number_index(doc_lengths, padded_pos)
    padded = jnp.concatenate([tail_rows, proj], axis=0)
    conv = short_convolution(padded, conv_weight, padded_document_ids, padded_pos, rows)
    query_part = conv[:, 0]
    product = (conv[:, 1] * conv[:, 2]).astype(jnp.bfloat16)

    swap_axis = ("mp", "zi")
    gathered = lax.all_to_all(product, swap_axis, split_axis=1, concat_axis=0, tiled=True)
    width = gathered.shape[1]
    gathered = gathered.reshape(mp_size, inner_size, rows, width).transpose(1, 0, 2, 3)
    gathered = gathered.reshape(inner_size * mp_size * rows, width)
    groups_here = residues.shape[0] // inner_size
    first_group = lax.axis_index("zi") * groups_here
    local_residues = lax.dynamic_slice_in_dim(residues, first_group, groups_here, 0)
    local_decays = lax.dynamic_slice_in_dim(decays, first_group, groups_here, 0)
    block_len = min(256, gathered.shape[0])
    filtered = long_filter(gathered, local_residues, local_decays, block_len, "zo")
    filtered = filtered.reshape(inner_size, mp_size, rows, width).transpose(1, 0, 2, 3)
    filtered = filtered.reshape(inner_size * mp_size * rows, width)
    filtered = lax.all_to_all(filtered, swap_axis, split_axis=0, concat_axis=1, tiled=True)
    return (query_part * filtered.astype(jnp.float32)).astype(jnp.bfloat16)


def solution(mesh):
    ctx_size, mp_size = mesh.devices.shape
    inner = 4 if ctx_size % 4 == 0 else 1
    split_mesh = Mesh(mesh.devices.reshape(ctx_size // inner, inner, mp_size), ("zo", "zi", "mp"))
    mapped = jax.shard_map(
        shards,
        mesh=split_mesh,
        in_specs=(P(("zo", "zi", "mp"), None, None), P(), P("mp", None), P("mp", None), P()),
        out_specs=P(("zo", "zi", "mp"), None),
        check_vma=False,
    )
    placed = NamedSharding(mesh, P(("ctx", "mp"), None))

    def run(*args):
        return lax.with_sharding_constraint(mapped(*args), placed)

    return run
```

```python
import jax
import jax.numpy as jnp
from jax import lax
from jax.sharding import Mesh, NamedSharding, PartitionSpec as P

HIGHEST = lax.Precision.HIGHEST
HIGH = lax.Precision.HIGH


def shifted(block, axis, distance):
    count = lax.axis_size(axis)
    route = [(i, i + distance) for i in range(count - distance)]
    return lax.ppermute(block, axis, route)


def document_number_index(doc_lengths, positions):
    doc_starts = jnp.cumsum(doc_lengths) - doc_lengths
    inside = (doc_starts[None, :] <= positions[:, None]).astype(jnp.int32)
    return jnp.sum(inside, axis=1) - 1


def short_convolution(padded, conv_weight, padded_document_ids, padded_pos, out_rows):
    kernel_len = conv_weight.shape[1]
    result = jnp.zeros((out_rows,) + padded.shape[1:], jnp.float32)
    own_docs = padded_document_ids[kernel_len - 1 :]
    for position_shift in range(kernel_len):
        begin_row = kernel_len - 1 - position_shift
        earlier = padded[begin_row : begin_row + out_rows].astype(jnp.float32)
        keep_mask = (padded_document_ids[begin_row : begin_row + out_rows] == own_docs) & (
            padded_pos[begin_row : begin_row + out_rows] >= 0
        )
        result = (
            result
            + conv_weight[:, position_shift, :][None]
            * earlier
            * keep_mask.astype(jnp.float32)[:, None, None]
        )
    return result


def split_product(form, weights, inputs):
    upper_part = weights.astype(jnp.bfloat16)
    lower_part = (weights - upper_part.astype(jnp.float32)).astype(jnp.bfloat16)
    first = jnp.einsum(form, upper_part, inputs, preferred_element_type=jnp.float32)
    return first + jnp.einsum(form, lower_part, inputs, preferred_element_type=jnp.float32)


def long_filter(product, residues, decays, block_len, outer_axis):
    positions, channels = product.shape
    group_count = residues.shape[0]
    group_width = channels // group_count
    block_count = positions // block_len
    coefficient = residues * jnp.sqrt(decays)
    offsets = jnp.arange(block_len, dtype=jnp.float32)
    left = coefficient[:, None, :] * jnp.exp(-decays[:, None, :] * offsets[None, :, None])
    right = jnp.exp(decays[:, :, None] * offsets[None, None, :])
    tile = jnp.einsum("grm,gms->grs", left, right, precision=HIGHEST)
    lag = jnp.arange(block_len)[:, None] - jnp.arange(block_len)[None, :]
    tile = jnp.where((lag >= 0)[None], tile, 0.0)
    inputs = product.reshape(block_count, block_len, group_count, group_width)
    intra = split_product("grs,bsgc->brgc", tile, inputs)

    end_weight = jnp.exp(-decays[:, :, None] * (float(block_len) - offsets)[None, None, :])
    block_state = split_product("gms,bsgc->gmbc", end_weight, inputs)

    blocks = jnp.arange(block_count, dtype=jnp.float32)
    to_end = jnp.exp(-decays[:, :, None] * (float(block_len) * (block_count - 1 - blocks))[None, None, :])
    run_state = jnp.einsum("gmb,gmbc->gmc", to_end, block_state, precision=HIGH)
    count = lax.axis_size(outer_axis)
    flat = run_state.reshape(1, -1)
    sent = jnp.broadcast_to(flat, (count, flat.shape[1]))
    gathered = lax.all_to_all(sent, outer_axis, split_axis=0, concat_axis=0, tiled=True)
    gathered = gathered.reshape((count,) + run_state.shape)
    here = lax.axis_index(outer_axis)
    earlier = jnp.arange(count, dtype=jnp.int32)
    gap = (here - 1 - earlier).astype(jnp.float32) * float(positions)
    weight = jnp.where(
        (earlier < here)[:, None, None],
        jnp.exp(-decays[None] * jnp.maximum(gap, 0.0)[:, None, None]),
        0.0,
    )
    incoming = jnp.sum(weight[:, :, :, None] * gathered, axis=0)

    later = jnp.arange(block_count)[:, None]
    before = jnp.arange(block_count)[None, :]
    block_gap = jnp.maximum(later - 1 - before, 0).astype(jnp.float32) * float(block_len)
    carry = jnp.where((before < later)[None, None], jnp.exp(-decays[:, :, None, None] * block_gap[None, None]), 0.0)
    state = jnp.einsum("gmab,gmbc->gmac", carry, block_state, precision=HIGH)
    partial = intra + jnp.einsum("grm,gmbc->brgc", left, state, precision=HIGH)

    start_decay = jnp.exp(-decays[:, :, None] * (float(block_len) * blocks)[None, None, :])
    run_left = left[:, None, :, :] * jnp.transpose(start_decay, (0, 2, 1))[:, :, None, :]
    outer = jnp.einsum("gbrm,gmc->brgc", run_left, incoming, precision=HIGH)
    return (partial + outer).reshape(positions, channels).astype(jnp.bfloat16)


def shards(proj, conv_weight, residues, decays, doc_lengths):
    kernel_len = conv_weight.shape[1]
    rows = proj.shape[0]
    outer_size = lax.axis_size("zo")
    inner_size = lax.axis_size("zi")
    mp_size = lax.axis_size("mp")
    lin_axis = ("zo", "zi", "mp")
    tail_rows = shifted(proj[rows - (kernel_len - 1) :], lin_axis, 1)
    lin_index = (lax.axis_index("zo") * inner_size + lax.axis_index("zi")) * mp_size + lax.axis_index("mp")
    padded_pos = lin_index * rows - (kernel_len - 1) + jnp.arange(rows + kernel_len - 1, dtype=jnp.int32)
    padded_document_ids = document_number_index(doc_lengths, padded_pos)
    padded = jnp.concatenate([tail_rows, proj], axis=0)
    conv = short_convolution(padded, conv_weight, padded_document_ids, padded_pos, rows)
    query_part = conv[:, 0]
    product = (conv[:, 1] * conv[:, 2]).astype(jnp.bfloat16)

    swap_axis = ("mp", "zi")
    gathered = lax.all_to_all(product, swap_axis, split_axis=1, concat_axis=0, tiled=True)
    width = gathered.shape[1]
    gathered = gathered.reshape(mp_size, inner_size, rows, width).transpose(1, 0, 2, 3)
    gathered = gathered.reshape(inner_size * mp_size * rows, width)
    groups_here = residues.shape[0] // inner_size
    first_group = lax.axis_index("zi") * groups_here
    local_residues = lax.dynamic_slice_in_dim(residues, first_group, groups_here, 0)
    local_decays = lax.dynamic_slice_in_dim(decays, first_group, groups_here, 0)
    block_len = min(256, gathered.shape[0])
    filtered = long_filter(gathered, local_residues, local_decays, block_len, "zo")
    filtered = filtered.reshape(inner_size, mp_size, rows, width).transpose(1, 0, 2, 3)
    filtered = filtered.reshape(inner_size * mp_size * rows, width)
    filtered = lax.all_to_all(filtered, swap_axis, split_axis=0, concat_axis=1, tiled=True)
    return (query_part * filtered.astype(jnp.float32)).astype(jnp.bfloat16)


def solution(mesh):
    ctx_size, mp_size = mesh.devices.shape
    inner = 4 if ctx_size % 4 == 0 else 1
    split_mesh = Mesh(mesh.devices.reshape(ctx_size // inner, inner, mp_size), ("zo", "zi", "mp"))
    mapped = jax.shard_map(
        shards,
        mesh=split_mesh,
        in_specs=(P(("zo", "zi", "mp"), None, None), P(), P("mp", None), P("mp", None), P()),
        out_specs=P(("zo", "zi", "mp"), None),
        check_vma=False,
    )
    placed = NamedSharding(mesh, P(("ctx", "mp"), None))

    def run(*args):
        return lax.with_sharding_constraint(mapped(*args), placed)

    return run
```

```python
import jax
import jax.numpy as jnp
from jax import lax
from jax.sharding import Mesh, NamedSharding, PartitionSpec as P

HIGHEST = lax.Precision.HIGHEST
HIGH = lax.Precision.HIGH


def shifted(block, axis, distance):
    count = lax.axis_size(axis)
    route = [(i, i + distance) for i in range(count - distance)]
    return lax.ppermute(block, axis, route)


def document_number_index(doc_lengths, positions):
    doc_starts = jnp.cumsum(doc_lengths) - doc_lengths
    inside = (doc_starts[None, :] <= positions[:, None]).astype(jnp.int32)
    return jnp.sum(inside, axis=1) - 1


def short_convolution(padded, conv_weight, padded_document_ids, padded_pos, out_rows):
    kernel_len = conv_weight.shape[1]
    result = jnp.zeros((out_rows,) + padded.shape[1:], jnp.float32)
    own_docs = padded_document_ids[kernel_len - 1 :]
    for position_shift in range(kernel_len):
        begin_row = kernel_len - 1 - position_shift
        earlier = padded[begin_row : begin_row + out_rows].astype(jnp.float32)
        keep_mask = (padded_document_ids[begin_row : begin_row + out_rows] == own_docs) & (
            padded_pos[begin_row : begin_row + out_rows] >= 0
        )
        result = (
            result
            + conv_weight[:, position_shift, :][None]
            * earlier
            * keep_mask.astype(jnp.float32)[:, None, None]
        )
    return result


def split_product(form, weights, inputs):
    upper_part = weights.astype(jnp.bfloat16)
    lower_part = (weights - upper_part.astype(jnp.float32)).astype(jnp.bfloat16)
    first = jnp.einsum(form, upper_part, inputs, preferred_element_type=jnp.float32)
    return first + jnp.einsum(form, lower_part, inputs, preferred_element_type=jnp.float32)


def long_filter(product, residues, decays, block_len, outer_axis):
    positions, channels = product.shape
    group_count = residues.shape[0]
    group_width = channels // group_count
    block_count = positions // block_len
    coefficient = residues * jnp.sqrt(decays)
    offsets = jnp.arange(block_len, dtype=jnp.float32)
    left = coefficient[:, None, :] * jnp.exp(-decays[:, None, :] * offsets[None, :, None])
    right = jnp.exp(decays[:, :, None] * offsets[None, None, :])
    tile = jnp.einsum("grm,gms->grs", left, right, precision=HIGHEST)
    lag = jnp.arange(block_len)[:, None] - jnp.arange(block_len)[None, :]
    tile = jnp.where((lag >= 0)[None], tile, 0.0)
    inputs = product.reshape(block_count, block_len, group_count, group_width)
    intra = split_product("grs,bsgc->brgc", tile, inputs)

    end_weight = jnp.exp(-decays[:, :, None] * (float(block_len) - offsets)[None, None, :])
    block_state = split_product("gms,bsgc->gmbc", end_weight, inputs)

    blocks = jnp.arange(block_count, dtype=jnp.float32)
    to_end = jnp.exp(-decays[:, :, None] * (float(block_len) * (block_count - 1 - blocks))[None, None, :])
    run_state = jnp.einsum("gmb,gmbc->gmc", to_end, block_state, precision=HIGH)
    count = lax.axis_size(outer_axis)
    flat = run_state.reshape(1, -1)
    sent = jnp.broadcast_to(flat, (count, flat.shape[1]))
    gathered = lax.all_to_all(sent, outer_axis, split_axis=0, concat_axis=0, tiled=True)
    gathered = gathered.reshape((count,) + run_state.shape)
    here = lax.axis_index(outer_axis)
    earlier = jnp.arange(count, dtype=jnp.int32)
    gap = (here - 1 - earlier).astype(jnp.float32) * float(positions)
    weight = jnp.where(
        (earlier < here)[:, None, None],
        jnp.exp(-decays[None] * jnp.maximum(gap, 0.0)[:, None, None]),
        0.0,
    )
    incoming = jnp.sum(weight[:, :, :, None] * gathered, axis=0)

    later = jnp.arange(block_count)[:, None]
    before = jnp.arange(block_count)[None, :]
    block_gap = jnp.maximum(later - 1 - before, 0).astype(jnp.float32) * float(block_len)
    carry = jnp.where((before < later)[None, None], jnp.exp(-decays[:, :, None, None] * block_gap[None, None]), 0.0)
    state = jnp.einsum("gmab,gmbc->gmac", carry, block_state, precision=HIGH)
    partial = intra + jnp.einsum("grm,gmbc->brgc", left, state, precision=HIGH)

    start_decay = jnp.exp(-decays[:, :, None] * (float(block_len) * blocks)[None, None, :])
    run_left = left[:, None, :, :] * jnp.transpose(start_decay, (0, 2, 1))[:, :, None, :]
    outer = jnp.einsum("gbrm,gmc->brgc", run_left, incoming, precision=HIGH)
    return (partial + outer).reshape(positions, channels).astype(jnp.bfloat16)


def shards(proj, conv_weight, residues, decays, doc_lengths):
    kernel_len = conv_weight.shape[1]
    rows = proj.shape[0]
    outer_size = lax.axis_size("zo")
    inner_size = lax.axis_size("zi")
    mp_size = lax.axis_size("mp")
    lin_axis = ("zo", "zi", "mp")
    tail_rows = shifted(proj[rows - (kernel_len - 1) :], lin_axis, 1)
    lin_index = (lax.axis_index("zo") * inner_size + lax.axis_index("zi")) * mp_size + lax.axis_index("mp")
    padded_pos = lin_index * rows - (kernel_len - 1) + jnp.arange(rows + kernel_len - 1, dtype=jnp.int32)
    padded_document_ids = document_number_index(doc_lengths, padded_pos)
    padded = jnp.concatenate([tail_rows, proj], axis=0)
    pair = short_convolution(padded[:, 1:], conv_weight[1:], padded_document_ids, padded_pos, rows)
    product = (pair[:, 0] * pair[:, 1]).astype(jnp.bfloat16)

    swap_axis = ("mp", "zi")
    gathered = lax.all_to_all(product, swap_axis, split_axis=1, concat_axis=0, tiled=True)
    width = gathered.shape[1]
    gathered = gathered.reshape(mp_size, inner_size, rows, width).transpose(1, 0, 2, 3)
    gathered = gathered.reshape(inner_size * mp_size * rows, width)
    groups_here = residues.shape[0] // inner_size
    first_group = lax.axis_index("zi") * groups_here
    local_residues = lax.dynamic_slice_in_dim(residues, first_group, groups_here, 0)
    local_decays = lax.dynamic_slice_in_dim(decays, first_group, groups_here, 0)
    block_len = min(256, gathered.shape[0])
    filtered = long_filter(gathered, local_residues, local_decays, block_len, "zo")
    filtered = filtered.reshape(inner_size, mp_size, rows, width).transpose(1, 0, 2, 3)
    filtered = filtered.reshape(inner_size * mp_size * rows, width)
    filtered = lax.all_to_all(filtered, swap_axis, split_axis=0, concat_axis=1, tiled=True)
    query_part = short_convolution(padded[:, :1], conv_weight[:1], padded_document_ids, padded_pos, rows)[:, 0]
    return (query_part * filtered.astype(jnp.float32)).astype(jnp.bfloat16)


def solution(mesh):
    ctx_size, mp_size = mesh.devices.shape
    inner = 4 if ctx_size % 4 == 0 else 1
    split_mesh = Mesh(mesh.devices.reshape(ctx_size // inner, inner, mp_size), ("zo", "zi", "mp"))
    mapped = jax.shard_map(
        shards,
        mesh=split_mesh,
        in_specs=(P(("zo", "zi", "mp"), None, None), P(), P("mp", None), P("mp", None), P()),
        out_specs=P(("zo", "zi", "mp"), None),
        check_vma=False,
    )
    placed = NamedSharding(mesh, P(("ctx", "mp"), None))

    def run(*args):
        return lax.with_sharding_constraint(mapped(*args), placed)

    return run
```

```python
import jax
import jax.numpy as jnp
from jax import lax
from jax.sharding import Mesh, NamedSharding, PartitionSpec as P

HIGHEST = lax.Precision.HIGHEST
HIGH = lax.Precision.HIGH


def shifted(block, axis, distance):
    count = lax.axis_size(axis)
    route = [(i, i + distance) for i in range(count - distance)]
    return lax.ppermute(block, axis, route)


def document_number_index(doc_lengths, positions):
    doc_starts = jnp.cumsum(doc_lengths) - doc_lengths
    inside = (doc_starts[None, :] <= positions[:, None]).astype(jnp.int32)
    return jnp.sum(inside, axis=1) - 1


def short_convolution(padded, conv_weight, padded_document_ids, padded_pos, out_rows):
    kernel_len = conv_weight.shape[1]
    result = jnp.zeros((out_rows,) + padded.shape[1:], jnp.float32)
    own_docs = padded_document_ids[kernel_len - 1 :]
    for position_shift in range(kernel_len):
        begin_row = kernel_len - 1 - position_shift
        earlier = padded[begin_row : begin_row + out_rows].astype(jnp.float32)
        keep_mask = (padded_document_ids[begin_row : begin_row + out_rows] == own_docs) & (
            padded_pos[begin_row : begin_row + out_rows] >= 0
        )
        result = (
            result
            + conv_weight[:, position_shift, :][None]
            * earlier
            * keep_mask.astype(jnp.float32)[:, None, None]
        )
    return result


def split_product(form, weights, inputs):
    upper_part = weights.astype(jnp.bfloat16)
    lower_part = (weights - upper_part.astype(jnp.float32)).astype(jnp.bfloat16)
    first = jnp.einsum(form, upper_part, inputs, preferred_element_type=jnp.float32)
    return first + jnp.einsum(form, lower_part, inputs, preferred_element_type=jnp.float32)


def long_filter(product, residues, decays, block_len, outer_axis):
    positions, channels = product.shape
    group_count = residues.shape[0]
    group_width = channels // group_count
    block_count = positions // block_len
    coefficient = residues * jnp.sqrt(decays)
    offsets = jnp.arange(block_len, dtype=jnp.float32)
    left = coefficient[:, None, :] * jnp.exp(-decays[:, None, :] * offsets[None, :, None])
    right = jnp.exp(decays[:, :, None] * offsets[None, None, :])
    tile = jnp.einsum("grm,gms->grs", left, right, precision=HIGHEST)
    lag = jnp.arange(block_len)[:, None] - jnp.arange(block_len)[None, :]
    tile = jnp.where((lag >= 0)[None], tile, 0.0)
    inputs = product.reshape(block_count, block_len, group_count, group_width)
    intra = split_product("grs,bsgc->brgc", tile, inputs)

    end_weight = jnp.exp(-decays[:, :, None] * (float(block_len) - offsets)[None, None, :])
    block_state = split_product("gms,bsgc->gmbc", end_weight, inputs)

    blocks = jnp.arange(block_count, dtype=jnp.float32)
    to_end = jnp.exp(-decays[:, :, None] * (float(block_len) * (block_count - 1 - blocks))[None, None, :])
    run_state = jnp.einsum("gmb,gmbc->gmc", to_end, block_state, precision=HIGH)
    count = lax.axis_size(outer_axis)
    flat = run_state.reshape(1, -1)
    sent = jnp.broadcast_to(flat, (count, flat.shape[1]))
    gathered = lax.all_to_all(sent, outer_axis, split_axis=0, concat_axis=0, tiled=True)
    gathered = gathered.reshape((count,) + run_state.shape)
    here = lax.axis_index(outer_axis)
    earlier = jnp.arange(count, dtype=jnp.int32)
    gap = (here - 1 - earlier).astype(jnp.float32) * float(positions)
    weight = jnp.where(
        (earlier < here)[:, None, None],
        jnp.exp(-decays[None] * jnp.maximum(gap, 0.0)[:, None, None]),
        0.0,
    )
    incoming = jnp.sum(weight[:, :, :, None] * gathered, axis=0)

    later = jnp.arange(block_count)[:, None]
    before = jnp.arange(block_count)[None, :]
    block_gap = jnp.maximum(later - 1 - before, 0).astype(jnp.float32) * float(block_len)
    carry = jnp.where((before < later)[None, None], jnp.exp(-decays[:, :, None, None] * block_gap[None, None]), 0.0)
    state = jnp.einsum("gmab,gmbc->gmac", carry, block_state, precision=HIGH)
    partial = intra + jnp.einsum("grm,gmbc->brgc", left, state, precision=HIGH)

    start_decay = jnp.exp(-decays[:, :, None] * (float(block_len) * blocks)[None, None, :])
    run_left = left[:, None, :, :] * jnp.transpose(start_decay, (0, 2, 1))[:, :, None, :]
    outer = jnp.einsum("gbrm,gmc->brgc", run_left, incoming, precision=HIGH)
    return (partial + outer).reshape(positions, channels).astype(jnp.bfloat16)


def shards(proj, conv_weight, residues, decays, doc_lengths):
    kernel_len = conv_weight.shape[1]
    rows = proj.shape[0]
    outer_size = lax.axis_size("zo")
    inner_size = lax.axis_size("zi")
    mp_size = lax.axis_size("mp")
    lin_axis = ("zo", "zi", "mp")
    tail_rows = shifted(proj[rows - (kernel_len - 1) :], lin_axis, 1)
    lin_index = (lax.axis_index("zo") * inner_size + lax.axis_index("zi")) * mp_size + lax.axis_index("mp")
    padded_pos = lin_index * rows - (kernel_len - 1) + jnp.arange(rows + kernel_len - 1, dtype=jnp.int32)
    padded_document_ids = document_number_index(doc_lengths, padded_pos)
    padded = jnp.concatenate([tail_rows, proj], axis=0)
    pair = short_convolution(padded[:, 1:], conv_weight[1:], padded_document_ids, padded_pos, rows)
    product = (pair[:, 0] * pair[:, 1]).astype(jnp.bfloat16)

    swap_axis = ("mp", "zi")
    gathered = lax.all_to_all(product, swap_axis, split_axis=1, concat_axis=0, tiled=True)
    query_part = short_convolution(padded[:, :1], conv_weight[:1], padded_document_ids, padded_pos, rows)[:, 0]
    gathered, query_part = lax.optimization_barrier((gathered, query_part))
    width = gathered.shape[1]
    gathered = gathered.reshape(mp_size, inner_size, rows, width).transpose(1, 0, 2, 3)
    gathered = gathered.reshape(inner_size * mp_size * rows, width)
    groups_here = residues.shape[0] // inner_size
    first_group = lax.axis_index("zi") * groups_here
    local_residues = lax.dynamic_slice_in_dim(residues, first_group, groups_here, 0)
    local_decays = lax.dynamic_slice_in_dim(decays, first_group, groups_here, 0)
    block_len = min(256, gathered.shape[0])
    filtered = long_filter(gathered, local_residues, local_decays, block_len, "zo")
    filtered = filtered.reshape(inner_size, mp_size, rows, width).transpose(1, 0, 2, 3)
    filtered = filtered.reshape(inner_size * mp_size * rows, width)
    filtered = lax.all_to_all(filtered, swap_axis, split_axis=0, concat_axis=1, tiled=True)
    return (query_part * filtered.astype(jnp.float32)).astype(jnp.bfloat16)


def solution(mesh):
    ctx_size, mp_size = mesh.devices.shape
    inner = 4 if ctx_size % 4 == 0 else 1
    split_mesh = Mesh(mesh.devices.reshape(ctx_size // inner, inner, mp_size), ("zo", "zi", "mp"))
    mapped = jax.shard_map(
        shards,
        mesh=split_mesh,
        in_specs=(P(("zo", "zi", "mp"), None, None), P(), P("mp", None), P("mp", None), P()),
        out_specs=P(("zo", "zi", "mp"), None),
        check_vma=False,
    )
    placed = NamedSharding(mesh, P(("ctx", "mp"), None))

    def run(*args):
        return lax.with_sharding_constraint(mapped(*args), placed)

    return run
```

```python
import jax
import jax.numpy as jnp
from jax import lax
from jax.sharding import Mesh, NamedSharding, PartitionSpec as P

HIGHEST = lax.Precision.HIGHEST
HIGH = lax.Precision.HIGH


def shifted(block, axis, distance):
    count = lax.axis_size(axis)
    route = [(i, i + distance) for i in range(count - distance)]
    return lax.ppermute(block, axis, route)


def document_number_index(doc_lengths, positions):
    doc_starts = jnp.cumsum(doc_lengths) - doc_lengths
    inside = (doc_starts[None, :] <= positions[:, None]).astype(jnp.int32)
    return jnp.sum(inside, axis=1) - 1


def short_convolution(padded, conv_weight, padded_document_ids, padded_pos, out_rows):
    kernel_len = conv_weight.shape[1]
    result = jnp.zeros((out_rows,) + padded.shape[1:], jnp.float32)
    own_docs = padded_document_ids[kernel_len - 1 :]
    for position_shift in range(kernel_len):
        begin_row = kernel_len - 1 - position_shift
        earlier = padded[begin_row : begin_row + out_rows].astype(jnp.float32)
        keep_mask = (padded_document_ids[begin_row : begin_row + out_rows] == own_docs) & (
            padded_pos[begin_row : begin_row + out_rows] >= 0
        )
        result = (
            result
            + conv_weight[:, position_shift, :][None]
            * earlier
            * keep_mask.astype(jnp.float32)[:, None, None]
        )
    return result


def split_product(form, weights, inputs):
    upper_part = weights.astype(jnp.bfloat16)
    lower_part = (weights - upper_part.astype(jnp.float32)).astype(jnp.bfloat16)
    first = jnp.einsum(form, upper_part, inputs, preferred_element_type=jnp.float32)
    return first + jnp.einsum(form, lower_part, inputs, preferred_element_type=jnp.float32)


def long_filter(product, residues, decays, block_len, outer_axis):
    positions, channels = product.shape
    group_count = residues.shape[0]
    group_width = channels // group_count
    block_count = positions // block_len
    coefficient = residues * jnp.sqrt(decays)
    offsets = jnp.arange(block_len, dtype=jnp.float32)
    left = coefficient[:, None, :] * jnp.exp(-decays[:, None, :] * offsets[None, :, None])
    right = jnp.exp(decays[:, :, None] * offsets[None, None, :])
    tile = jnp.einsum("grm,gms->grs", left, right, precision=HIGHEST)
    lag = jnp.arange(block_len)[:, None] - jnp.arange(block_len)[None, :]
    tile = jnp.where((lag >= 0)[None], tile, 0.0)
    inputs = product.reshape(block_count, block_len, group_count, group_width)
    intra = split_product("grs,bsgc->brgc", tile, inputs)

    end_weight = jnp.exp(-decays[:, :, None] * (float(block_len) - offsets)[None, None, :])
    block_state = split_product("gms,bsgc->gmbc", end_weight, inputs)

    blocks = jnp.arange(block_count, dtype=jnp.float32)
    run_offsets = jnp.arange(positions, dtype=jnp.float32).reshape(block_count, block_len)
    run_weight = jnp.exp(-decays[:, :, None, None] * (float(positions) - run_offsets)[None, None])
    run_state = split_product("gmbs,bsgc->gmc", run_weight, inputs)
    count = lax.axis_size(outer_axis)
    flat = run_state.reshape(1, -1)
    sent = jnp.broadcast_to(flat, (count, flat.shape[1]))
    gathered = lax.all_to_all(sent, outer_axis, split_axis=0, concat_axis=0, tiled=True)
    gathered = gathered.reshape((count,) + run_state.shape)
    here = lax.axis_index(outer_axis)
    earlier = jnp.arange(count, dtype=jnp.int32)
    gap = (here - 1 - earlier).astype(jnp.float32) * float(positions)
    weight = jnp.where(
        (earlier < here)[:, None, None],
        jnp.exp(-decays[None] * jnp.maximum(gap, 0.0)[:, None, None]),
        0.0,
    )
    incoming = jnp.sum(weight[:, :, :, None] * gathered, axis=0)

    later = jnp.arange(block_count)[:, None]
    before = jnp.arange(block_count)[None, :]
    block_gap = jnp.maximum(later - 1 - before, 0).astype(jnp.float32) * float(block_len)
    carry = jnp.where((before < later)[None, None], jnp.exp(-decays[:, :, None, None] * block_gap[None, None]), 0.0)
    state = jnp.einsum("gmab,gmbc->gmac", carry, block_state, precision=HIGH)
    partial = intra + jnp.einsum("grm,gmbc->brgc", left, state, precision=HIGH)

    start_decay = jnp.exp(-decays[:, :, None] * (float(block_len) * blocks)[None, None, :])
    run_left = left[:, None, :, :] * jnp.transpose(start_decay, (0, 2, 1))[:, :, None, :]
    outer = jnp.einsum("gbrm,gmc->brgc", run_left, incoming, precision=HIGH)
    return (partial + outer).reshape(positions, channels).astype(jnp.bfloat16)


def shards(proj, conv_weight, residues, decays, doc_lengths):
    kernel_len = conv_weight.shape[1]
    rows = proj.shape[0]
    inner_size = lax.axis_size("zi")
    mp_size = lax.axis_size("mp")
    lin_axis = ("zo", "zi", "mp")
    tail_rows = shifted(proj[rows - (kernel_len - 1) :], lin_axis, 1)
    lin_index = (lax.axis_index("zo") * inner_size + lax.axis_index("zi")) * mp_size + lax.axis_index("mp")
    padded_pos = lin_index * rows - (kernel_len - 1) + jnp.arange(rows + kernel_len - 1, dtype=jnp.int32)
    padded_document_ids = document_number_index(doc_lengths, padded_pos)
    padded = jnp.concatenate([tail_rows, proj], axis=0)
    conv = short_convolution(padded, conv_weight, padded_document_ids, padded_pos, rows)
    query_part = conv[:, 0]
    product = (conv[:, 1] * conv[:, 2]).astype(jnp.bfloat16)

    swap_axis = ("mp", "zi")
    gathered = lax.all_to_all(product, swap_axis, split_axis=1, concat_axis=0, tiled=True)
    width = gathered.shape[1]
    gathered = gathered.reshape(mp_size, inner_size, rows, width).transpose(1, 0, 2, 3)
    gathered = gathered.reshape(inner_size * mp_size * rows, width)
    groups_here = residues.shape[0] // inner_size
    first_group = lax.axis_index("zi") * groups_here
    local_residues = lax.dynamic_slice_in_dim(residues, first_group, groups_here, 0)
    local_decays = lax.dynamic_slice_in_dim(decays, first_group, groups_here, 0)
    block_len = min(256, gathered.shape[0])
    filtered = long_filter(gathered, local_residues, local_decays, block_len, "zo")
    filtered = filtered.reshape(inner_size, mp_size, rows, width).transpose(1, 0, 2, 3)
    filtered = filtered.reshape(inner_size * mp_size * rows, width)
    filtered = lax.all_to_all(filtered, swap_axis, split_axis=0, concat_axis=1, tiled=True)
    return (query_part * filtered.astype(jnp.float32)).astype(jnp.bfloat16)


def solution(mesh):
    ctx_size, mp_size = mesh.devices.shape
    inner = 4 if ctx_size % 4 == 0 else 1
    split_mesh = Mesh(mesh.devices.reshape(ctx_size // inner, inner, mp_size), ("zo", "zi", "mp"))
    mapped = jax.shard_map(
        shards,
        mesh=split_mesh,
        in_specs=(P(("zo", "zi", "mp"), None, None), P(), P("mp", None), P("mp", None), P()),
        out_specs=P(("zo", "zi", "mp"), None),
        check_vma=False,
    )
    placed = NamedSharding(mesh, P(("ctx", "mp"), None))

    def run(*args):
        return lax.with_sharding_constraint(mapped(*args), placed)

    return run
```

```python
import jax
import jax.numpy as jnp
from jax import lax
from jax.sharding import Mesh, NamedSharding, PartitionSpec as P

HIGHEST = lax.Precision.HIGHEST
HIGH = lax.Precision.HIGH


def shifted(block, axis, distance):
    count = lax.axis_size(axis)
    route = [(i, i + distance) for i in range(count - distance)]
    return lax.ppermute(block, axis, route)


def document_number_index(doc_lengths, positions):
    doc_starts = jnp.cumsum(doc_lengths) - doc_lengths
    inside = (doc_starts[None, :] <= positions[:, None]).astype(jnp.int32)
    return jnp.sum(inside, axis=1) - 1


def short_convolution(padded, conv_weight, padded_document_ids, padded_pos, out_rows):
    kernel_len = conv_weight.shape[1]
    result = jnp.zeros((out_rows,) + padded.shape[1:], jnp.float32)
    own_docs = padded_document_ids[kernel_len - 1 :]
    for position_shift in range(kernel_len):
        begin_row = kernel_len - 1 - position_shift
        earlier = padded[begin_row : begin_row + out_rows].astype(jnp.float32)
        keep_mask = (padded_document_ids[begin_row : begin_row + out_rows] == own_docs) & (
            padded_pos[begin_row : begin_row + out_rows] >= 0
        )
        result = (
            result
            + conv_weight[:, position_shift, :][None]
            * earlier
            * keep_mask.astype(jnp.float32)[:, None, None]
        )
    return result


def split_product(form, weights, inputs):
    upper_part = weights.astype(jnp.bfloat16)
    lower_part = (weights - upper_part.astype(jnp.float32)).astype(jnp.bfloat16)
    first = jnp.einsum(form, upper_part, inputs, preferred_element_type=jnp.float32)
    return first + jnp.einsum(form, lower_part, inputs, preferred_element_type=jnp.float32)


def long_filter(product, residues, decays, block_len, outer_axis, run_state):
    positions, channels = product.shape
    group_count = residues.shape[0]
    group_width = channels // group_count
    block_count = positions // block_len
    coefficient = residues * jnp.sqrt(decays)
    offsets = jnp.arange(block_len, dtype=jnp.float32)
    left = coefficient[:, None, :] * jnp.exp(-decays[:, None, :] * offsets[None, :, None])
    right = jnp.exp(decays[:, :, None] * offsets[None, None, :])
    tile = jnp.einsum("grm,gms->grs", left, right, precision=HIGHEST)
    lag = jnp.arange(block_len)[:, None] - jnp.arange(block_len)[None, :]
    tile = jnp.where((lag >= 0)[None], tile, 0.0)
    inputs = product.reshape(block_count, block_len, group_count, group_width)
    intra = split_product("grs,bsgc->brgc", tile, inputs)

    end_weight = jnp.exp(-decays[:, :, None] * (float(block_len) - offsets)[None, None, :])
    block_state = split_product("gms,bsgc->gmbc", end_weight, inputs)

    blocks = jnp.arange(block_count, dtype=jnp.float32)
    count = lax.axis_size(outer_axis)
    flat = run_state.reshape(1, -1)
    sent = jnp.broadcast_to(flat, (count, flat.shape[1]))
    gathered = lax.all_to_all(sent, outer_axis, split_axis=0, concat_axis=0, tiled=True)
    gathered = gathered.reshape((count,) + run_state.shape)
    here = lax.axis_index(outer_axis)
    earlier = jnp.arange(count, dtype=jnp.int32)
    gap = (here - 1 - earlier).astype(jnp.float32) * float(positions)
    weight = jnp.where(
        (earlier < here)[:, None, None],
        jnp.exp(-decays[None] * jnp.maximum(gap, 0.0)[:, None, None]),
        0.0,
    )
    incoming = jnp.sum(weight[:, :, :, None] * gathered, axis=0)

    later = jnp.arange(block_count)[:, None]
    before = jnp.arange(block_count)[None, :]
    block_gap = jnp.maximum(later - 1 - before, 0).astype(jnp.float32) * float(block_len)
    carry = jnp.where((before < later)[None, None], jnp.exp(-decays[:, :, None, None] * block_gap[None, None]), 0.0)
    state = jnp.einsum("gmab,gmbc->gmac", carry, block_state, precision=HIGH)
    partial = intra + jnp.einsum("grm,gmbc->brgc", left, state, precision=HIGH)

    start_decay = jnp.exp(-decays[:, :, None] * (float(block_len) * blocks)[None, None, :])
    run_left = left[:, None, :, :] * jnp.transpose(start_decay, (0, 2, 1))[:, :, None, :]
    outer = jnp.einsum("gbrm,gmc->brgc", run_left, incoming, precision=HIGH)
    return (partial + outer).reshape(positions, channels).astype(jnp.bfloat16)


def shards(proj, conv_weight, residues, decays, doc_lengths):
    kernel_len = conv_weight.shape[1]
    rows = proj.shape[0]
    inner_size = lax.axis_size("zi")
    mp_size = lax.axis_size("mp")
    lin_axis = ("zo", "zi", "mp")
    tail_rows = shifted(proj[rows - (kernel_len - 1) :], lin_axis, 1)
    lin_index = (lax.axis_index("zo") * inner_size + lax.axis_index("zi")) * mp_size + lax.axis_index("mp")
    padded_pos = lin_index * rows - (kernel_len - 1) + jnp.arange(rows + kernel_len - 1, dtype=jnp.int32)
    padded_document_ids = document_number_index(doc_lengths, padded_pos)
    padded = jnp.concatenate([tail_rows, proj], axis=0)
    pair = short_convolution(padded[:, 1:], conv_weight[1:], padded_document_ids, padded_pos, rows)
    product = (pair[:, 0] * pair[:, 1]).astype(jnp.bfloat16)

    swap_axis = ("mp", "zi")
    gathered = lax.all_to_all(product, swap_axis, split_axis=1, concat_axis=0, tiled=True)
    query_part = short_convolution(padded[:, :1], conv_weight[:1], padded_document_ids, padded_pos, rows)[:, 0]
    gathered, query_part = lax.optimization_barrier((gathered, query_part))
    width = gathered.shape[1]
    groups_here = residues.shape[0] // inner_size
    first_group = lax.axis_index("zi") * groups_here
    local_residues = lax.dynamic_slice_in_dim(residues, first_group, groups_here, 0)
    local_decays = lax.dynamic_slice_in_dim(decays, first_group, groups_here, 0)
    arrived = gathered.reshape(mp_size, inner_size, rows, groups_here, width // groups_here)
    position_of = (
        jnp.arange(inner_size, dtype=jnp.float32)[None, :, None] * float(mp_size * rows)
        + jnp.arange(mp_size, dtype=jnp.float32)[:, None, None] * float(rows)
        + jnp.arange(rows, dtype=jnp.float32)[None, None, :]
    )
    run_weight = jnp.exp(
        -local_decays[:, :, None, None, None] * (float(inner_size * mp_size * rows) - position_of)[None, None]
    )
    run_state = split_product("gmabr,abrgc->gmc", run_weight, arrived)
    gathered = gathered.reshape(mp_size, inner_size, rows, width).transpose(1, 0, 2, 3)
    gathered = gathered.reshape(inner_size * mp_size * rows, width)
    block_len = min(256, gathered.shape[0])
    filtered = long_filter(gathered, local_residues, local_decays, block_len, "zo", run_state)
    filtered = filtered.reshape(inner_size, mp_size, rows, width).transpose(1, 0, 2, 3)
    filtered = filtered.reshape(inner_size * mp_size * rows, width)
    filtered = lax.all_to_all(filtered, swap_axis, split_axis=0, concat_axis=1, tiled=True)
    return (query_part * filtered.astype(jnp.float32)).astype(jnp.bfloat16)


def solution(mesh):
    ctx_size, mp_size = mesh.devices.shape
    inner = 4 if ctx_size % 4 == 0 else 1
    split_mesh = Mesh(mesh.devices.reshape(ctx_size // inner, inner, mp_size), ("zo", "zi", "mp"))
    mapped = jax.shard_map(
        shards,
        mesh=split_mesh,
        in_specs=(P(("zo", "zi", "mp"), None, None), P(), P("mp", None), P("mp", None), P()),
        out_specs=P(("zo", "zi", "mp"), None),
        check_vma=False,
    )
    placed = NamedSharding(mesh, P(("ctx", "mp"), None))

    def run(*args):
        return lax.with_sharding_constraint(mapped(*args), placed)

    return run
```

```python
import jax
import jax.numpy as jnp
from jax import lax
from jax.sharding import Mesh, NamedSharding, PartitionSpec as P

HIGHEST = lax.Precision.HIGHEST
HIGH = lax.Precision.HIGH


def shifted(block, axis, distance):
    count = lax.axis_size(axis)
    route = [(i, i + distance) for i in range(count - distance)]
    return lax.ppermute(block, axis, route)


def document_number_index(doc_lengths, positions):
    doc_starts = jnp.cumsum(doc_lengths) - doc_lengths
    inside = (doc_starts[None, :] <= positions[:, None]).astype(jnp.int32)
    return jnp.sum(inside, axis=1) - 1


def short_convolution(padded, conv_weight, padded_document_ids, padded_pos, out_rows):
    kernel_len = conv_weight.shape[1]
    result = jnp.zeros((out_rows,) + padded.shape[1:], jnp.float32)
    own_docs = padded_document_ids[kernel_len - 1 :]
    for position_shift in range(kernel_len):
        begin_row = kernel_len - 1 - position_shift
        earlier = padded[begin_row : begin_row + out_rows].astype(jnp.float32)
        keep_mask = (padded_document_ids[begin_row : begin_row + out_rows] == own_docs) & (
            padded_pos[begin_row : begin_row + out_rows] >= 0
        )
        result = (
            result
            + conv_weight[:, position_shift, :][None]
            * earlier
            * keep_mask.astype(jnp.float32)[:, None, None]
        )
    return result


def split_product(form, weights, inputs):
    upper_part = weights.astype(jnp.bfloat16)
    lower_part = (weights - upper_part.astype(jnp.float32)).astype(jnp.bfloat16)
    first = jnp.einsum(form, upper_part, inputs, preferred_element_type=jnp.float32)
    return first + jnp.einsum(form, lower_part, inputs, preferred_element_type=jnp.float32)


def long_filter(product, residues, decays, block_len, outer_axis):
    positions, channels = product.shape
    group_count = residues.shape[0]
    group_width = channels // group_count
    block_count = positions // block_len
    coefficient = residues * jnp.sqrt(decays)
    offsets = jnp.arange(block_len, dtype=jnp.float32)
    left = coefficient[:, None, :] * jnp.exp(-decays[:, None, :] * offsets[None, :, None])
    right = jnp.exp(decays[:, :, None] * offsets[None, None, :])
    tile = jnp.einsum("grm,gms->grs", left, right, precision=HIGHEST)
    lag = jnp.arange(block_len)[:, None] - jnp.arange(block_len)[None, :]
    tile = jnp.where((lag >= 0)[None], tile, 0.0)
    inputs = product.reshape(block_count, block_len, group_count, group_width)
    intra = split_product("grs,bsgc->brgc", tile, inputs)

    end_weight = jnp.exp(-decays[:, :, None] * (float(block_len) - offsets)[None, None, :])
    block_state = split_product("gms,bsgc->gmbc", end_weight, inputs)

    blocks = jnp.arange(block_count, dtype=jnp.float32)
    run_offsets = jnp.arange(positions, dtype=jnp.float32).reshape(block_count, block_len)
    run_weight = jnp.exp(-decays[:, :, None, None] * (float(positions) - run_offsets)[None, None])
    run_state = split_product("gmbs,bsgc->gmc", run_weight, inputs)
    count = lax.axis_size(outer_axis)
    flat = run_state.reshape(1, -1)
    sent = jnp.broadcast_to(flat, (count, flat.shape[1]))
    gathered = lax.all_to_all(sent, outer_axis, split_axis=0, concat_axis=0, tiled=True)
    gathered = gathered.reshape((count,) + run_state.shape)
    here = lax.axis_index(outer_axis)
    earlier = jnp.arange(count, dtype=jnp.int32)
    gap = (here - 1 - earlier).astype(jnp.float32) * float(positions)
    weight = jnp.where(
        (earlier < here)[:, None, None],
        jnp.exp(-decays[None] * jnp.maximum(gap, 0.0)[:, None, None]),
        0.0,
    )
    incoming = jnp.sum(weight[:, :, :, None] * gathered, axis=0)

    later = jnp.arange(block_count)[:, None]
    before = jnp.arange(block_count)[None, :]
    block_gap = jnp.maximum(later - 1 - before, 0).astype(jnp.float32) * float(block_len)
    carry = jnp.where((before < later)[None, None], jnp.exp(-decays[:, :, None, None] * block_gap[None, None]), 0.0)
    state = jnp.einsum("gmab,gmbc->gmac", carry, block_state, precision=HIGH)
    partial = lax.optimization_barrier(intra + jnp.einsum("grm,gmbc->brgc", left, state, precision=HIGH))

    start_decay = jnp.exp(-decays[:, :, None] * (float(block_len) * blocks)[None, None, :])
    run_left = left[:, None, :, :] * jnp.transpose(start_decay, (0, 2, 1))[:, :, None, :]
    outer = jnp.einsum("gbrm,gmc->brgc", run_left, incoming, precision=HIGH)
    return (partial + outer).reshape(positions, channels).astype(jnp.bfloat16)


def shards(proj, conv_weight, residues, decays, doc_lengths):
    kernel_len = conv_weight.shape[1]
    rows = proj.shape[0]
    inner_size = lax.axis_size("zi")
    mp_size = lax.axis_size("mp")
    lin_axis = ("zo", "zi", "mp")
    tail_rows = shifted(proj[rows - (kernel_len - 1) :], lin_axis, 1)
    lin_index = (lax.axis_index("zo") * inner_size + lax.axis_index("zi")) * mp_size + lax.axis_index("mp")
    padded_pos = lin_index * rows - (kernel_len - 1) + jnp.arange(rows + kernel_len - 1, dtype=jnp.int32)
    padded_document_ids = document_number_index(doc_lengths, padded_pos)
    padded = jnp.concatenate([tail_rows, proj], axis=0)
    pair = short_convolution(padded[:, 1:], conv_weight[1:], padded_document_ids, padded_pos, rows)
    product = (pair[:, 0] * pair[:, 1]).astype(jnp.bfloat16)

    swap_axis = ("mp", "zi")
    gathered = lax.all_to_all(product, swap_axis, split_axis=1, concat_axis=0, tiled=True)
    query_part = short_convolution(padded[:, :1], conv_weight[:1], padded_document_ids, padded_pos, rows)[:, 0]
    gathered, query_part = lax.optimization_barrier((gathered, query_part))
    width = gathered.shape[1]
    gathered = gathered.reshape(mp_size, inner_size, rows, width).transpose(1, 0, 2, 3)
    gathered = gathered.reshape(inner_size * mp_size * rows, width)
    groups_here = residues.shape[0] // inner_size
    first_group = lax.axis_index("zi") * groups_here
    local_residues = lax.dynamic_slice_in_dim(residues, first_group, groups_here, 0)
    local_decays = lax.dynamic_slice_in_dim(decays, first_group, groups_here, 0)
    block_len = min(256, gathered.shape[0])
    filtered = long_filter(gathered, local_residues, local_decays, block_len, "zo")
    filtered = filtered.reshape(inner_size, mp_size, rows, width).transpose(1, 0, 2, 3)
    filtered = filtered.reshape(inner_size * mp_size * rows, width)
    filtered = lax.all_to_all(filtered, swap_axis, split_axis=0, concat_axis=1, tiled=True)
    return (query_part * filtered.astype(jnp.float32)).astype(jnp.bfloat16)


def solution(mesh):
    ctx_size, mp_size = mesh.devices.shape
    inner = 4 if ctx_size % 4 == 0 else 1
    split_mesh = Mesh(mesh.devices.reshape(ctx_size // inner, inner, mp_size), ("zo", "zi", "mp"))
    mapped = jax.shard_map(
        shards,
        mesh=split_mesh,
        in_specs=(P(("zo", "zi", "mp"), None, None), P(), P("mp", None), P("mp", None), P()),
        out_specs=P(("zo", "zi", "mp"), None),
        check_vma=False,
    )
    placed = NamedSharding(mesh, P(("ctx", "mp"), None))

    def run(*args):
        return lax.with_sharding_constraint(mapped(*args), placed)

    return run
```
